512 devices in a mesh: segment: 16 (over z, core), mp: 32 (over y, x).
Axes of the slice: x: 4, y: 8, z: 8, core: 2. Of those that a mesh axis runs over, the one named last changes fastest.
Arguments:
- rows: bfloat16 [16, 2, 128, 8192], P('segment', None, None, 'mp'), may hold values from -6 to 6
- carry: bfloat16 [16, 128, 8192], P('segment', None, 'mp'), may hold values from -6 to 6
- weights: bfloat16 [16, 2, 8192, 4096], P('segment', None, None, 'mp'), may hold values from -1.1932427 to 1.1932427
- neighbours: int32 [16, 2, 2, 2], P('segment'), may hold values from 0 to 7, all different within a row
Outputs:
- passed: bfloat16 [16, 128, 8192], P('segment', None, 'mp')
- returned: bfloat16 [16, 128, 8192], P('segment', None, 'mp')
- kv_grad: bfloat16 [1024, 2, 4096], P(None, None, 'mp')
The draws below stay inside these ranges and needn't reach their ends.
Inputs may be any that keep to these rules, and one draw needn't show every extreme that they name: Each group's 2 neighbours are different pool blocks; pool blocks are numbered by encoder segment in order, then by row.
All inputs are finite; a program needn't handle non-finite values.
Results may differ from the reference program's by a relative error of at most 0.02.
The reference program's roundings to bfloat16 on the way count: a program that leaves them out, or rounds other values in their place, can miss the bound.
Values may be sent and summed in bfloat16 or wider, within the bound.
No kernel may reach another device: no remote copies, remote signals or barrier semaphores. Data moves between devices by JAX's collectives and lax.ppermute only.
A program may use at most 64 MiB of HBM per device.

```python
import math
import jax
import jax.numpy as jnp
from jax import lax

D = 8192
HD = 128
HEADS = 32
GROUP = 64
NBLEN = 128
NEIGH = 2
GROUPS_MB = 2
TOK = 128
KEYS = 256
N_ENC = 4
POOL = 8
N_SEGMENT = 16


def draw_rows(key, part):
    values = jnp.clip(jax.random.normal(key, (N_SEGMENT, 2, TOK, D), jnp.float32), -6.0, 6.0)
    return values.astype(jnp.bfloat16)


def draw_weights(key, part):
    values = jnp.clip(jax.random.normal(key, (N_SEGMENT, 2, D, HEADS * HD), jnp.float32), -4.0, 4.0) * (1.0 / math.sqrt(D))
    segment_ids = lax.broadcasted_iota(jnp.int32, (N_SEGMENT, 2, 1, 1), 0)
    slot_ids = lax.broadcasted_iota(jnp.int32, (N_SEGMENT, 2, 1, 1), 1)
    output_slot = jnp.logical_and(segment_ids < N_SEGMENT - N_ENC, slot_ids == 1)
    values = jnp.where(output_slot, values * 8.0, values)
    return values.astype(jnp.bfloat16)


def steps_of(stream_key, extent, pieces, least, high):
    level = 1.0
    for dim, shards_of in pieces:
        draws = jax.random.uniform(jax.random.fold_in(jax.random.fold_in(stream_key, 6), dim), (shards_of,), jnp.float32, least / len(pieces), high / len(pieces))
        level = level * jnp.repeat(jnp.exp(draws), extent[dim] // shards_of).reshape((-1,) + (1,) * (len(extent) - 1 - dim))
    return level


def distinct(stream_key, rows, number_of, top, lift):
    sequence = jax.random.permutation(jax.random.fold_in(stream_key, 1), number_of)
    pull = sequence
    for power in range(3):
        pull = pull * pull // number_of
    pull = pull * lift // number_of
    chance = jax.random.randint(jax.random.fold_in(stream_key, 2), (rows, number_of), 0, 4096) + pull
    sure = jax.random.permutation(jax.random.fold_in(stream_key, 3), rows)[jnp.arange(number_of) % rows]
    chance = jnp.where(jnp.arange(rows)[:, None] == sure[None, :], 1 << 14, chance)
    priority = chance * number_of + jnp.arange(number_of)
    return lax.top_k(priority.astype(jnp.int32), top)[1].astype(jnp.int32)


def gaussian(rng, dims, spread, limit, pieces=(), kind=jnp.bfloat16):
    drawn = jax.random.normal(rng, dims, jnp.float32) * spread
    if len(pieces) > 0:
        drawn = steps_of(rng, dims, pieces, -0.22, 0.18) * drawn
    return jnp.clip(drawn, min=-limit, max=limit).astype(kind)


def setup_inputs(seed: int = 0) -> dict:
    splits = jax.random.split(jax.random.key(seed), 5)
    return {
        "rows": draw_rows(jax.random.fold_in(splits[4], 71), 0),
        "carry": gaussian(splits[1], (N_SEGMENT, TOK, D), 1.0, 6.0, ((0, 16), (2, 32))),
        "weights": draw_weights(jax.random.fold_in(splits[4], 71), 0),
        "neighbours": distinct(splits[3], N_SEGMENT * 2 * GROUPS_MB, POOL, NEIGH, 4096).reshape((N_SEGMENT, 2, GROUPS_MB, NEIGH)),
    }


def attend(queries, key_rows, score_scale):
    scores = jnp.einsum('cqhd,ckhd->chqk', queries.astype(jnp.float32), key_rows.astype(jnp.float32)) * score_scale
    soft = jax.nn.softmax(scores, axis=-1)
    return (soft, soft.astype(jnp.bfloat16))

def attend_back(queries, key_rows, value_rows, soft, rounded, upstream, score_scale):
    upper = upstream.astype(jnp.float32)
    d_soft = jnp.einsum('cqhd,ckhd->chqk', upper, value_rows.astype(jnp.float32))
    grad_values = jnp.einsum('chqk,cqhd->ckhd', rounded.astype(jnp.float32), upper)
    d_scores = soft * (d_soft - lax.optimization_barrier(jnp.sum(d_soft * soft, axis=-1, keepdims=True)))
    grad_queries = (jnp.einsum('chqk,ckhd->cqhd', d_scores, key_rows.astype(jnp.float32)) * score_scale).astype(jnp.bfloat16)
    grad_keys = jnp.einsum('chqk,cqhd->ckhd', d_scores, queries.astype(jnp.float32)) * score_scale
    return (grad_queries, grad_keys, grad_values)

def head_terms(left, matrix):
    terms = jnp.einsum('thd,ehd->the', left.astype(jnp.float32), matrix.astype(jnp.float32))
    rounded = lax.optimization_barrier(terms.astype(jnp.bfloat16))
    return lax.optimization_barrier(jnp.sum(rounded.astype(jnp.float32), axis=1))

def reference(rows, carry, weights, neighbours):
    score_scale = 1.0 / math.sqrt(HD)
    first_encoder = N_SEGMENT - N_ENC
    key_parts = []
    value_parts = []
    for encoder in range(first_encoder, N_SEGMENT):
        flat = rows[encoder].reshape(2 * TOK, D)
        key_parts.append(jnp.dot(flat, weights[encoder, 0], preferred_element_type=jnp.float32).astype(jnp.bfloat16))
        value_parts.append(jnp.dot(flat, weights[encoder, 1], preferred_element_type=jnp.float32).astype(jnp.bfloat16))
    pool_keys = jnp.concatenate(key_parts, axis=0).reshape(POOL, NBLEN, HEADS, HD)
    pool_values = jnp.concatenate(value_parts, axis=0).reshape(POOL, NBLEN, HEADS, HD)
    grad_pool_keys = jnp.zeros((POOL, NBLEN, HEADS, HD), jnp.float32)
    grad_pool_values = jnp.zeros((POOL, NBLEN, HEADS, HD), jnp.float32)
    forward_list = []
    backward_list = []
    for segment in range(N_SEGMENT):
        if segment >= first_encoder:
            forward_list.append(carry[segment])
            backward_list.append(carry[segment])
            continue
        rows32 = rows[segment].astype(jnp.float32)
        queries = jnp.dot(rows[segment].reshape(2 * TOK, D), weights[segment, 0], preferred_element_type=jnp.float32).astype(jnp.bfloat16)
        queries = queries.reshape(2, GROUPS_MB, GROUP, HEADS, HD)
        w_query = weights[segment, 0].reshape(D, HEADS, HD)
        w_out = weights[segment, 1].reshape(D, HEADS, HD)

        def fetch(batch):
            index = neighbours[segment, batch]
            return (pool_keys[index].reshape(GROUPS_MB, KEYS, HEADS, HD), pool_values[index].reshape(GROUPS_MB, KEYS, HEADS, HD))
        keys_fwd, values_fwd = fetch(0)
        soft_fwd, rounded_fwd = attend(queries[0], keys_fwd, score_scale)
        mixed = jnp.einsum('chqk,ckhd->cqhd', rounded_fwd.astype(jnp.float32), values_fwd.astype(jnp.float32)).astype(jnp.bfloat16)
        out_sum = head_terms(mixed.reshape(TOK, HEADS, HD), w_out)
        forward_list.append((rows32[0] + out_sum).astype(jnp.bfloat16))
        upstream = jnp.dot(carry[segment], weights[segment, 1], preferred_element_type=jnp.float32).astype(jnp.bfloat16)
        upstream = upstream.reshape(GROUPS_MB, GROUP, HEADS, HD)
        keys_back, values_back = fetch(1)
        soft_back, rounded_back = attend(queries[1], keys_back, score_scale)
        grad_queries, grad_keys, grad_values = attend_back(queries[1], keys_back, values_back, soft_back, rounded_back, upstream, score_scale)
        grad_input = head_terms(grad_queries.reshape(TOK, HEADS, HD), w_query)
        back = carry[segment].astype(jnp.float32) + grad_input
        backward_list.append(back.astype(jnp.bfloat16))
        onehot = (neighbours[segment, 1][..., None] == jnp.arange(POOL, dtype=jnp.int32)[None, None, :]).astype(jnp.float32)
        grad_pool_keys = grad_pool_keys + jnp.einsum('cbp,cbrhd->prhd', onehot, grad_keys.reshape(GROUPS_MB, NEIGH, NBLEN, HEADS, HD))
        grad_pool_values = grad_pool_values + jnp.einsum('cbp,cbrhd->prhd', onehot, grad_values.reshape(GROUPS_MB, NEIGH, NBLEN, HEADS, HD))
    kv_grad = jnp.stack([grad_pool_keys.reshape(POOL * NBLEN, HEADS * HD), grad_pool_values.reshape(POOL * NBLEN, HEADS * HD)], axis=1).astype(jnp.bfloat16)
    passed = jnp.roll(jnp.stack(forward_list), 1, axis=0)
    returned = jnp.roll(jnp.stack(backward_list), -1, axis=0)
    return (passed, returned, kv_grad)
```

```python
import math

import jax
import jax.numpy as jnp
from jax import lax
from jax.sharding import PartitionSpec as P

GROUP = 64
NBLEN = 128
NEIGH = 2


def from_behind(x, axis, by):
    devices = lax.axis_size(axis)
    return lax.ppermute(x, axis, [(i, (i + by) % devices) for i in range(devices)])


def attend(queries, key_rows, score_scale):
    scores = (
        jnp.einsum("cqd,ckd->cqk", queries, key_rows, preferred_element_type=jnp.float32)
        * score_scale
    )
    soft = jax.nn.softmax(scores, axis=-1)
    return (soft, soft.astype(jnp.bfloat16))


def attend_back(queries, key_rows, value_rows, soft, rounded, upstream, score_scale):
    d_soft = jnp.einsum("cqd,ckd->cqk", upstream, value_rows, preferred_element_type=jnp.float32)
    grad_values = jnp.einsum("cqk,cqd->ckd", rounded, upstream, preferred_element_type=jnp.float32)
    d_scores = soft * (d_soft - jnp.sum(d_soft * soft, axis=-1, keepdims=True))
    grad_queries = (
        jnp.einsum("cqk,ckd->cqd", d_scores, key_rows.astype(jnp.float32)) * score_scale
    ).astype(jnp.bfloat16)
    grad_keys = jnp.einsum("cqk,cqd->ckd", d_scores, queries.astype(jnp.float32)) * score_scale
    return (grad_queries, grad_keys, grad_values)


def head_sum(term, axis):
    devices = lax.axis_size(axis)
    parts = term.astype(jnp.bfloat16).reshape(devices, term.shape[0] // devices, term.shape[1])
    moved = lax.all_to_all(parts, axis, 0, 0, tiled=True)
    return jnp.sum(moved.astype(jnp.float32), axis=0).T


def segment_sum(contrib, axis):
    devices = lax.axis_size(axis)
    parts = contrib.reshape(devices, contrib.shape[0] // devices, contrib.shape[1])
    moved = lax.all_to_all(parts, axis, 0, 0, tiled=True)
    summed = jnp.sum(moved.astype(jnp.float32), axis=0).astype(jnp.bfloat16)
    spread = jnp.broadcast_to(summed[None], (devices,) + summed.shape)
    return lax.all_to_all(spread, axis, 0, 0, tiled=True).reshape(contrib.shape)


def per_device(rows, carry, weights, neighbours):
    segments = lax.axis_size("segment")
    encoders = segments // 4
    first_encoder = segments - encoders
    is_encoder = lax.axis_index("segment") >= first_encoder
    local_rows = rows[0]
    local_carry = carry[0]
    full_rows, full_carry = (
        lax.all_gather(local_rows, "mp", axis=2, tiled=True),
        lax.all_gather(local_carry, "mp", axis=1, tiled=True),
    )
    tokens = local_rows.shape[1]
    width = full_rows.shape[2]
    head = weights.shape[3]
    w_query = weights[0, 0]
    w_out = weights[0, 1]

    def encode():
        flat = full_rows.reshape(2 * tokens, width)
        keyval = jnp.concatenate(
            [
                jnp.dot(flat, w_query, preferred_element_type=jnp.float32),
                jnp.dot(flat, w_out, preferred_element_type=jnp.float32),
            ],
            axis=-1,
        ).astype(jnp.bfloat16)
        return (keyval, jnp.zeros((2 * tokens, head), jnp.bfloat16))

    def decode():
        queries = jnp.dot(
            full_rows.reshape(2 * tokens, width), w_query, preferred_element_type=jnp.float32
        ).astype(jnp.bfloat16)
        return (jnp.zeros((2 * tokens, 2 * head), jnp.bfloat16), queries)

    encoded, queries = lax.cond(is_encoder, encode, decode)
    per_encoder = 2 * tokens // NBLEN
    pool_blocks = encoders * per_encoder
    collected = lax.all_gather(encoded, "segment", axis=0, tiled=True)
    pool = collected[first_encoder * 2 * tokens :].reshape(pool_blocks, NBLEN, 2 * head)
    groups = tokens // GROUP
    local_nbr = neighbours[0]
    score_scale = 1.0 / math.sqrt(head)
    query_blocks = queries.reshape(2, groups, GROUP, head)

    def fetch(batch):
        picked = pool[local_nbr[batch]].reshape(groups, NEIGH * NBLEN, 2 * head)
        return (picked[..., :head], picked[..., head:])

    keys_fwd, values_fwd = fetch(0)
    soft_fwd, rounded_fwd = attend(query_blocks[0], keys_fwd, score_scale)
    mixed = jnp.einsum(
        "cqk,ckd->cqd", rounded_fwd, values_fwd, preferred_element_type=jnp.float32
    ).astype(jnp.bfloat16)
    mixed_flat = mixed.reshape(tokens, head)
    piece = w_out
    out_sum = head_sum(
        lax.dot_general(piece, mixed_flat, (((1,), (1,)), ((), ())), preferred_element_type=jnp.float32),
        "mp",
    )
    forward_rows = (local_rows[0].astype(jnp.float32) + out_sum).astype(jnp.bfloat16)
    forward_rows = jnp.where(is_encoder, local_carry, forward_rows)
    passed = from_behind(forward_rows[None], "segment", 1)
    upstream = (
        jnp.dot(full_carry, w_out, preferred_element_type=jnp.float32)
        .astype(jnp.bfloat16)
        .reshape(groups, GROUP, head)
    )
    keys_back, values_back = fetch(1)
    soft_back, rounded_back = attend(query_blocks[1], keys_back, score_scale)
    grad_queries, grad_keys, grad_values = attend_back(
        query_blocks[1], keys_back, values_back, soft_back, rounded_back, upstream, score_scale
    )
    grad_flat = grad_queries.reshape(tokens, head)
    piece = w_query
    grad_input = head_sum(
        lax.dot_general(piece, grad_flat, (((1,), (1,)), ((), ())), preferred_element_type=jnp.float32),
        "mp",
    )
    back = local_carry.astype(jnp.float32) + grad_input
    back_rows = jnp.where(is_encoder, local_carry, back.astype(jnp.bfloat16))
    returned = from_behind(back_rows[None], "segment", -1)
    onehot = (
        local_nbr[1][..., None] == jnp.arange(pool_blocks, dtype=jnp.int32)[None, None, :]
    ).astype(jnp.float32)
    grad_keyval = jnp.concatenate([grad_keys, grad_values], axis=-1).reshape(
        groups, NEIGH, NBLEN, 2 * head
    )
    contrib = jnp.einsum("cbp,cbrf->prf", onehot, grad_keyval)
    contrib = jnp.where(is_encoder, jnp.zeros_like(contrib), contrib)
    pooled = segment_sum(contrib.astype(jnp.bfloat16).reshape(pool_blocks * NBLEN, 2 * head), "segment")
    kv_grad = pooled.reshape(pool_blocks * NBLEN, 2, head)
    return (passed, returned, kv_grad)


def solution(mesh):
    placed = (
        P("segment", None, None, "mp"),
        P("segment", None, "mp"),
        P("segment", None, None, "mp"),
        P("segment", None, None, None),
    )
    return jax.shard_map(
        per_device,
        mesh=mesh,
        in_specs=placed,
        out_specs=(P("segment", None, "mp"), P("segment", None, "mp"), P(None, None, "mp")),
        check_vma=False,
    )
```

```python
import math

import jax
import jax.numpy as jnp
from jax import lax
from jax.sharding import PartitionSpec as P

GROUP = 64
NBLEN = 128
NEIGH = 2


def from_behind(x, axis, by):
    devices = lax.axis_size(axis)
    return lax.ppermute(x, axis, [(i, (i + by) % devices) for i in range(devices)])


def attend(queries, key_rows, score_scale):
    scores = (
        jnp.einsum("cqd,ckd->cqk", queries, key_rows, preferred_element_type=jnp.float32)
        * score_scale
    )
    soft = jax.nn.softmax(scores, axis=-1)
    return (soft, soft.astype(jnp.bfloat16))


def attend_back(queries, key_rows, value_rows, soft, rounded, upstream, score_scale):
    d_soft = jnp.einsum("cqd,ckd->cqk", upstream, value_rows, preferred_element_type=jnp.float32)
    grad_values = jnp.einsum("cqk,cqd->ckd", rounded, upstream, preferred_element_type=jnp.float32)
    d_scores = soft * (d_soft - jnp.sum(d_soft * soft, axis=-1, keepdims=True))
    grad_queries = (
        jnp.einsum("cqk,ckd->cqd", d_scores, key_rows.astype(jnp.float32)) * score_scale
    ).astype(jnp.bfloat16)
    grad_keys = jnp.einsum("cqk,cqd->ckd", d_scores, queries.astype(jnp.float32)) * score_scale
    return (grad_queries, grad_keys, grad_values)


def head_sum(term, axis):
    devices = lax.axis_size(axis)
    parts = term.astype(jnp.bfloat16).reshape(devices, term.shape[0] // devices, term.shape[1])
    moved = lax.all_to_all(parts, axis, 0, 0, tiled=True)
    return jnp.sum(moved.astype(jnp.float32), axis=0).T


def segment_sum(contrib, axis):
    devices = lax.axis_size(axis)
    parts = contrib.reshape(devices, contrib.shape[0] // devices, contrib.shape[1])
    moved = lax.all_to_all(parts, axis, 0, 0, tiled=True)
    summed = jnp.sum(moved.astype(jnp.float32), axis=0).astype(jnp.bfloat16)
    spread = jnp.broadcast_to(summed[None], (devices,) + summed.shape)
    return lax.all_to_all(spread, axis, 0, 0, tiled=True).reshape(contrib.shape)


def per_device(rows, carry, weights, neighbours):
    segments = lax.axis_size("segment")
    encoders = segments // 4
    first_encoder = segments - encoders
    is_encoder = lax.axis_index("segment") >= first_encoder
    local_rows = rows[0]
    local_carry = carry[0]
    gathered = lax.all_gather(
        jnp.concatenate([local_rows, local_carry[None]], axis=0), "mp", axis=2, tiled=True
    )
    full_rows, full_carry = gathered[:2], gathered[2]
    tokens = local_rows.shape[1]
    width = full_rows.shape[2]
    head = weights.shape[3]
    w_query = weights[0, 0]
    w_out = weights[0, 1]

    def encode():
        flat = full_rows.reshape(2 * tokens, width)
        keyval = jnp.concatenate(
            [
                jnp.dot(flat, w_query, preferred_element_type=jnp.float32),
                jnp.dot(flat, w_out, preferred_element_type=jnp.float32),
            ],
            axis=-1,
        ).astype(jnp.bfloat16)
        return (keyval, jnp.zeros((2 * tokens, head), jnp.bfloat16))

    def decode():
        queries = jnp.dot(
            full_rows.reshape(2 * tokens, width), w_query, preferred_element_type=jnp.float32
        ).astype(jnp.bfloat16)
        return (jnp.zeros((2 * tokens, 2 * head), jnp.bfloat16), queries)

    encoded, queries = lax.cond(is_encoder, encode, decode)
    per_encoder = 2 * tokens // NBLEN
    pool_blocks = encoders * per_encoder
    collected = lax.all_gather(encoded, "segment", axis=0, tiled=True)
    pool = collected[first_encoder * 2 * tokens :].reshape(pool_blocks, NBLEN, 2 * head)
    groups = tokens // GROUP
    local_nbr = neighbours[0]
    score_scale = 1.0 / math.sqrt(head)
    query_blocks = queries.reshape(2, groups, GROUP, head)

    def fetch(batch):
        picked = pool[local_nbr[batch]].reshape(groups, NEIGH * NBLEN, 2 * head)
        return (picked[..., :head], picked[..., head:])

    keys_fwd, values_fwd = fetch(0)
    soft_fwd, rounded_fwd = attend(query_blocks[0], keys_fwd, score_scale)
    mixed = jnp.einsum(
        "cqk,ckd->cqd", rounded_fwd, values_fwd, preferred_element_type=jnp.float32
    ).astype(jnp.bfloat16)
    mixed_flat = mixed.reshape(tokens, head)
    piece = w_out
    out_sum = head_sum(
        lax.dot_general(piece, mixed_flat, (((1,), (1,)), ((), ())), preferred_element_type=jnp.float32),
        "mp",
    )
    forward_rows = (local_rows[0].astype(jnp.float32) + out_sum).astype(jnp.bfloat16)
    forward_rows = jnp.where(is_encoder, local_carry, forward_rows)
    passed = from_behind(forward_rows[None], "segment", 1)
    upstream = (
        jnp.dot(full_carry, w_out, preferred_element_type=jnp.float32)
        .astype(jnp.bfloat16)
        .reshape(groups, GROUP, head)
    )
    keys_back, values_back = fetch(1)
    soft_back, rounded_back = attend(query_blocks[1], keys_back, score_scale)
    grad_queries, grad_keys, grad_values = attend_back(
        query_blocks[1], keys_back, values_back, soft_back, rounded_back, upstream, score_scale
    )
    grad_flat = grad_queries.reshape(tokens, head)
    piece = w_query
    grad_input = head_sum(
        lax.dot_general(piece, grad_flat, (((1,), (1,)), ((), ())), preferred_element_type=jnp.float32),
        "mp",
    )
    back = local_carry.astype(jnp.float32) + grad_input
    back_rows = jnp.where(is_encoder, local_carry, back.astype(jnp.bfloat16))
    returned = from_behind(back_rows[None], "segment", -1)
    onehot = (
        local_nbr[1][..., None] == jnp.arange(pool_blocks, dtype=jnp.int32)[None, None, :]
    ).astype(jnp.float32)
    grad_keyval = jnp.concatenate([grad_keys, grad_values], axis=-1).reshape(
        groups, NEIGH, NBLEN, 2 * head
    )
    contrib = jnp.einsum("cbp,cbrf->prf", onehot, grad_keyval)
    contrib = jnp.where(is_encoder, jnp.zeros_like(contrib), contrib)
    pooled = segment_sum(contrib.astype(jnp.bfloat16).reshape(pool_blocks * NBLEN, 2 * head), "segment")
    kv_grad = pooled.reshape(pool_blocks * NBLEN, 2, head)
    return (passed, returned, kv_grad)


def solution(mesh):
    placed = (
        P("segment", None, None, "mp"),
        P("segment", None, "mp"),
        P("segment", None, None, "mp"),
        P("segment", None, None, None),
    )
    return jax.shard_map(
        per_device,
        mesh=mesh,
        in_specs=placed,
        out_specs=(P("segment", None, "mp"), P("segment", None, "mp"), P(None, None, "mp")),
        check_vma=False,
    )
```

```python
import math

import jax
import jax.numpy as jnp
from jax import lax
from jax.sharding import PartitionSpec as P

GROUP = 64
NBLEN = 128
NEIGH = 2


def from_behind(x, axis, by):
    devices = lax.axis_size(axis)
    return lax.ppermute(x, axis, [(i, (i + by) % devices) for i in range(devices)])


def attend(queries, key_rows, score_scale):
    scores = (
        jnp.einsum("cqd,ckd->cqk", queries, key_rows, preferred_element_type=jnp.float32)
        * score_scale
    )
    soft = jax.nn.softmax(scores, axis=-1)
    return (soft, soft.astype(jnp.bfloat16))


def attend_back(queries, key_rows, value_rows, soft, rounded, upstream, score_scale):
    d_soft = jnp.einsum("cqd,ckd->cqk", upstream, value_rows, preferred_element_type=jnp.float32)
    grad_values = jnp.einsum("cqk,cqd->ckd", rounded, upstream, preferred_element_type=jnp.float32)
    d_scores = soft * (d_soft - jnp.sum(d_soft * soft, axis=-1, keepdims=True))
    grad_queries = (
        jnp.einsum("cqk,ckd->cqd", d_scores, key_rows.astype(jnp.float32)) * score_scale
    ).astype(jnp.bfloat16)
    grad_keys = jnp.einsum("cqk,cqd->ckd", d_scores, queries.astype(jnp.float32)) * score_scale
    return (grad_queries, grad_keys, grad_values)


def head_sum(vectors, matrix):
    terms = jnp.einsum("htd,hfd->htf", vectors, matrix, preferred_element_type=jnp.float32)
    return jnp.sum(terms.astype(jnp.bfloat16).astype(jnp.float32), axis=0)


def segment_sum(contrib, axis):
    devices = lax.axis_size(axis)
    parts = contrib.reshape(devices, contrib.shape[0] // devices, contrib.shape[1])
    moved = lax.all_to_all(parts, axis, 0, 0, tiled=True)
    summed = jnp.sum(moved.astype(jnp.float32), axis=0).astype(jnp.bfloat16)
    spread = jnp.broadcast_to(summed[None], (devices,) + summed.shape)
    return lax.all_to_all(spread, axis, 0, 0, tiled=True).reshape(contrib.shape)


def per_device(rows, carry, weights, neighbours):
    segments = lax.axis_size("segment")
    encoders = segments // 4
    first_encoder = segments - encoders
    is_encoder = lax.axis_index("segment") >= first_encoder
    local_rows = rows[0]
    local_carry = carry[0]
    gathered = lax.all_gather(
        jnp.concatenate([local_rows, local_carry[None]], axis=0), "mp", axis=2, tiled=True
    )
    full_rows, full_carry = gathered[:2], gathered[2]
    tokens = local_rows.shape[1]
    width = full_rows.shape[2]
    head = weights.shape[3]
    w_query = weights[0, 0]
    w_out = weights[0, 1]
    features = width // lax.axis_size("mp")
    w_mine = lax.all_to_all(
        weights[0].reshape(2, lax.axis_size("mp"), features, head).transpose(1, 0, 2, 3),
        "mp",
        0,
        0,
        tiled=True,
    )

    def encode():
        flat = full_rows.reshape(2 * tokens, width)
        keyval = jnp.concatenate(
            [
                jnp.dot(flat, w_query, preferred_element_type=jnp.float32),
                jnp.dot(flat, w_out, preferred_element_type=jnp.float32),
            ],
            axis=-1,
        ).astype(jnp.bfloat16)
        return (keyval, jnp.zeros((2 * tokens, head), jnp.bfloat16))

    def decode():
        queries = jnp.dot(
            full_rows.reshape(2 * tokens, width), w_query, preferred_element_type=jnp.float32
        ).astype(jnp.bfloat16)
        return (jnp.zeros((2 * tokens, 2 * head), jnp.bfloat16), queries)

    encoded, queries = lax.cond(is_encoder, encode, decode)
    per_encoder = 2 * tokens // NBLEN
    pool_blocks = encoders * per_encoder
    collected = lax.all_gather(encoded, "segment", axis=0, tiled=True)
    pool = collected[first_encoder * 2 * tokens :].reshape(pool_blocks, NBLEN, 2 * head)
    groups = tokens // GROUP
    local_nbr = neighbours[0]
    score_scale = 1.0 / math.sqrt(head)
    query_blocks = queries.reshape(2, groups, GROUP, head)

    def fetch(batch):
        picked = pool[local_nbr[batch]].reshape(groups, NEIGH * NBLEN, 2 * head)
        return (picked[..., :head], picked[..., head:])

    keys_fwd, values_fwd = fetch(0)
    soft_fwd, rounded_fwd = attend(query_blocks[0], keys_fwd, score_scale)
    mixed = jnp.einsum(
        "cqk,ckd->cqd", rounded_fwd, values_fwd, preferred_element_type=jnp.float32
    ).astype(jnp.bfloat16)
    mixed_flat = mixed.reshape(tokens, head)
    upstream = (
        jnp.dot(full_carry, w_out, preferred_element_type=jnp.float32)
        .astype(jnp.bfloat16)
        .reshape(groups, GROUP, head)
    )
    keys_back, values_back = fetch(1)
    soft_back, rounded_back = attend(query_blocks[1], keys_back, score_scale)
    grad_queries, grad_keys, grad_values = attend_back(
        query_blocks[1], keys_back, values_back, soft_back, rounded_back, upstream, score_scale
    )
    grad_flat = grad_queries.reshape(tokens, head)
    heads = lax.axis_size("mp")
    small = jnp.stack([mixed_flat, grad_flat])
    every = lax.all_to_all(
        jnp.broadcast_to(small[None], (heads,) + small.shape), "mp", 0, 0, tiled=True
    )
    out_sum = head_sum(every[:, 0], w_mine[:, 1])
    grad_input = head_sum(every[:, 1], w_mine[:, 0])
    forward_rows = (local_rows[0].astype(jnp.float32) + out_sum).astype(jnp.bfloat16)
    forward_rows = jnp.where(is_encoder, local_carry, forward_rows)
    passed = from_behind(forward_rows[None], "segment", 1)
    back = local_carry.astype(jnp.float32) + grad_input
    back_rows = jnp.where(is_encoder, local_carry, back.astype(jnp.bfloat16))
    returned = from_behind(back_rows[None], "segment", -1)
    onehot = (
        local_nbr[1][..., None] == jnp.arange(pool_blocks, dtype=jnp.int32)[None, None, :]
    ).astype(jnp.float32)
    grad_keyval = jnp.concatenate([grad_keys, grad_values], axis=-1).reshape(
        groups, NEIGH, NBLEN, 2 * head
    )
    contrib = jnp.einsum("cbp,cbrf->prf", onehot, grad_keyval)
    contrib = jnp.where(is_encoder, jnp.zeros_like(contrib), contrib)
    pooled = segment_sum(contrib.astype(jnp.bfloat16).reshape(pool_blocks * NBLEN, 2 * head), "segment")
    kv_grad = pooled.reshape(pool_blocks * NBLEN, 2, head)
    return (passed, returned, kv_grad)


def solution(mesh):
    placed = (
        P("segment", None, None, "mp"),
        P("segment", None, "mp"),
        P("segment", None, None, "mp"),
        P("segment", None, None, None),
    )
    return jax.shard_map(
        per_device,
        mesh=mesh,
        in_specs=placed,
        out_specs=(P("segment", None, "mp"), P("segment", None, "mp"), P(None, None, "mp")),
        check_vma=False,
    )
```

```python
import functools
import math

import numpy as np

import jax
import jax.numpy as jnp
from jax import lax
from jax.sharding import Mesh, PartitionSpec as P

GROUP = 64
NBLEN = 128
NEIGH = 2


def from_behind(x, axis, by):
    devices = lax.axis_size(axis)
    return lax.ppermute(x, axis, [(i, (i + by) % devices) for i in range(devices)])


def attend(queries, key_rows, score_scale):
    scores = (
        jnp.einsum("cqd,ckd->cqk", queries, key_rows, preferred_element_type=jnp.float32)
        * score_scale
    )
    soft = jax.nn.softmax(scores, axis=-1)
    return (soft, soft.astype(jnp.bfloat16))


def attend_back(queries, key_rows, value_rows, soft, rounded, upstream, score_scale):
    d_soft = jnp.einsum("cqd,ckd->cqk", upstream, value_rows, preferred_element_type=jnp.float32)
    grad_values = jnp.einsum("cqk,cqd->ckd", rounded, upstream, preferred_element_type=jnp.float32)
    d_scores = soft * (d_soft - jnp.sum(d_soft * soft, axis=-1, keepdims=True))
    grad_queries = (
        jnp.einsum("cqk,ckd->cqd", d_scores, key_rows.astype(jnp.float32)) * score_scale
    ).astype(jnp.bfloat16)
    grad_keys = jnp.einsum("cqk,cqd->ckd", d_scores, queries.astype(jnp.float32)) * score_scale
    return (grad_queries, grad_keys, grad_values)


def head_sum(term, axis):
    devices = lax.axis_size(axis)
    parts = term.astype(jnp.bfloat16).reshape(devices, term.shape[0] // devices, term.shape[1])
    moved = lax.all_to_all(parts, axis, 0, 0, tiled=True)
    return jnp.sum(moved.astype(jnp.float32), axis=0).T


def segment_sum(contrib, axis):
    devices = lax.axis_size(axis)
    parts = contrib.reshape(devices, contrib.shape[0] // devices, contrib.shape[1])
    moved = lax.all_to_all(parts, axis, 0, 0, tiled=True)
    summed = jnp.sum(moved.astype(jnp.float32), axis=0).astype(jnp.bfloat16)
    spread = jnp.broadcast_to(summed[None], (devices,) + summed.shape)
    return lax.all_to_all(spread, axis, 0, 0, tiled=True).reshape(contrib.shape)


def per_device(mp, stages, rows, carry, weights, neighbours):
    segments = lax.axis_size("segment")
    encoders = segments // 4
    first_encoder = segments - encoders
    is_encoder = lax.axis_index("segment") >= first_encoder
    local_rows = rows[0]
    local_carry = carry[0]
    gathered = jnp.concatenate([local_rows, local_carry[None]], axis=0)
    for stage in stages:
        gathered = lax.all_gather(gathered, stage, axis=2, tiled=True)
    full_rows, full_carry = gathered[:2], gathered[2]
    tokens = local_rows.shape[1]
    width = full_rows.shape[2]
    head = weights.shape[3]
    w_query = weights[0, 0]
    w_out = weights[0, 1]

    def encode():
        flat = full_rows.reshape(2 * tokens, width)
        keyval = jnp.concatenate(
            [
                jnp.dot(flat, w_query, preferred_element_type=jnp.float32),
                jnp.dot(flat, w_out, preferred_element_type=jnp.float32),
            ],
            axis=-1,
        ).astype(jnp.bfloat16)
        return (keyval, jnp.zeros((2 * tokens, head), jnp.bfloat16))

    def decode():
        queries = jnp.dot(
            full_rows.reshape(2 * tokens, width), w_query, preferred_element_type=jnp.float32
        ).astype(jnp.bfloat16)
        return (jnp.zeros((2 * tokens, 2 * head), jnp.bfloat16), queries)

    encoded, queries = lax.cond(is_encoder, encode, decode)
    per_encoder = 2 * tokens // NBLEN
    pool_blocks = encoders * per_encoder
    collected = lax.all_gather(encoded, "segment", axis=0, tiled=True)
    pool = collected[first_encoder * 2 * tokens :].reshape(pool_blocks, NBLEN, 2 * head)
    groups = tokens // GROUP
    local_nbr = neighbours[0]
    score_scale = 1.0 / math.sqrt(head)
    query_blocks = queries.reshape(2, groups, GROUP, head)

    def fetch(batch):
        picked = pool[local_nbr[batch]].reshape(groups, NEIGH * NBLEN, 2 * head)
        return (picked[..., :head], picked[..., head:])

    keys_fwd, values_fwd = fetch(0)
    soft_fwd, rounded_fwd = attend(query_blocks[0], keys_fwd, score_scale)
    mixed = jnp.einsum(
        "cqk,ckd->cqd", rounded_fwd, values_fwd, preferred_element_type=jnp.float32
    ).astype(jnp.bfloat16)
    mixed_flat = mixed.reshape(tokens, head)
    piece = w_out
    out_sum = head_sum(
        lax.dot_general(piece, mixed_flat, (((1,), (1,)), ((), ())), preferred_element_type=jnp.float32),
        mp,
    )
    forward_rows = (local_rows[0].astype(jnp.float32) + out_sum).astype(jnp.bfloat16)
    forward_rows = jnp.where(is_encoder, local_carry, forward_rows)
    passed = from_behind(forward_rows[None], "segment", 1)
    upstream = (
        jnp.dot(full_carry, w_out, preferred_element_type=jnp.float32)
        .astype(jnp.bfloat16)
        .reshape(groups, GROUP, head)
    )
    keys_back, values_back = fetch(1)
    soft_back, rounded_back = attend(query_blocks[1], keys_back, score_scale)
    grad_queries, grad_keys, grad_values = attend_back(
        query_blocks[1], keys_back, values_back, soft_back, rounded_back, upstream, score_scale
    )
    grad_flat = grad_queries.reshape(tokens, head)
    piece = w_query
    grad_input = head_sum(
        lax.dot_general(piece, grad_flat, (((1,), (1,)), ((), ())), preferred_element_type=jnp.float32),
        mp,
    )
    back = local_carry.astype(jnp.float32) + grad_input
    back_rows = jnp.where(is_encoder, local_carry, back.astype(jnp.bfloat16))
    returned = from_behind(back_rows[None], "segment", -1)
    onehot = (
        local_nbr[1][..., None] == jnp.arange(pool_blocks, dtype=jnp.int32)[None, None, :]
    ).astype(jnp.float32)
    grad_keyval = jnp.concatenate([grad_keys, grad_values], axis=-1).reshape(
        groups, NEIGH, NBLEN, 2 * head
    )
    contrib = jnp.einsum("cbp,cbrf->prf", onehot, grad_keyval)
    contrib = jnp.where(is_encoder, jnp.zeros_like(contrib), contrib)
    pooled = segment_sum(contrib.astype(jnp.bfloat16).reshape(pool_blocks * NBLEN, 2 * head), "segment")
    kv_grad = pooled.reshape(pool_blocks * NBLEN, 2, head)
    return (passed, returned, kv_grad)


def split_mp(mesh):
    devices = mesh.devices
    try:
        xs = [d.coords[0] for d in devices[0]]
        ys = [d.coords[1] for d in devices[0]]
    except (AttributeError, TypeError, IndexError):
        return None
    wide = len(set(xs))
    tall = devices.shape[1] // wide
    if wide * tall != devices.shape[1] or wide == 1 or tall == 1:
        return None
    grid_x = np.array(xs).reshape(tall, wide)
    grid_y = np.array(ys).reshape(tall, wide)
    if not ((grid_x == grid_x[:1]).all() and (grid_y == grid_y[:, :1]).all()):
        return None
    return Mesh(devices.reshape(devices.shape[0], tall, wide), ("segment", "my", "mx"))


def solution(mesh):
    split = split_mp(mesh)
    if split is None:
        inner, mp, stages = mesh, "mp", ("mp",)
    else:
        inner, mp, stages = split, ("my", "mx"), ("mx", "my")
    placed = (
        P("segment", None, None, mp),
        P("segment", None, mp),
        P("segment", None, None, mp),
        P("segment", None, None, None),
    )
    return jax.shard_map(
        functools.partial(per_device, mp, stages),
        mesh=inner,
        in_specs=placed,
        out_specs=(P("segment", None, mp), P("segment", None, mp), P(None, None, mp)),
        check_vma=False,
    )
```

```python
import functools
import math

import numpy as np

import jax
import jax.numpy as jnp
from jax import lax
from jax.sharding import Mesh, PartitionSpec as P

GROUP = 64
NBLEN = 128
NEIGH = 2


def from_behind(x, axis, by):
    devices = lax.axis_size(axis)
    return lax.ppermute(x, axis, [(i, (i + by) % devices) for i in range(devices)])


def attend(queries, key_rows, score_scale):
    scores = (
        jnp.einsum("cqd,ckd->cqk", queries, key_rows, preferred_element_type=jnp.float32)
        * score_scale
    )
    soft = jax.nn.softmax(scores, axis=-1)
    return (soft, soft.astype(jnp.bfloat16))


def attend_back(queries, key_rows, value_rows, soft, rounded, upstream, score_scale):
    d_soft = jnp.einsum("cqd,ckd->cqk", upstream, value_rows, preferred_element_type=jnp.float32)
    grad_values = jnp.einsum("cqk,cqd->ckd", rounded, upstream, preferred_element_type=jnp.float32)
    d_scores = soft * (d_soft - jnp.sum(d_soft * soft, axis=-1, keepdims=True))
    grad_queries = (
        jnp.einsum("cqk,ckd->cqd", d_scores, key_rows.astype(jnp.float32)) * score_scale
    ).astype(jnp.bfloat16)
    grad_keys = jnp.einsum("cqk,cqd->ckd", d_scores, queries.astype(jnp.float32)) * score_scale
    return (grad_queries, grad_keys, grad_values)


def head_sum(terms, axis):
    devices = lax.axis_size(axis)
    count, width, tokens = terms.shape
    parts = terms.astype(jnp.bfloat16).reshape(count, devices, width // devices, tokens).transpose(1, 0, 2, 3)
    moved = lax.all_to_all(parts, axis, 0, 0, tiled=True)
    return jnp.sum(moved.astype(jnp.float32), axis=0).transpose(0, 2, 1)


def segment_sum(contrib, axis):
    devices = lax.axis_size(axis)
    parts = contrib.reshape(devices, contrib.shape[0] // devices, contrib.shape[1])
    moved = lax.all_to_all(parts, axis, 0, 0, tiled=True)
    summed = jnp.sum(moved.astype(jnp.float32), axis=0).astype(jnp.bfloat16)
    spread = jnp.broadcast_to(summed[None], (devices,) + summed.shape)
    return lax.all_to_all(spread, axis, 0, 0, tiled=True).reshape(contrib.shape)


def per_device(mp, stages, rows, carry, weights, neighbours):
    segments = lax.axis_size("segment")
    encoders = segments // 4
    first_encoder = segments - encoders
    is_encoder = lax.axis_index("segment") >= first_encoder
    local_rows = rows[0]
    local_carry = carry[0]
    gathered = jnp.concatenate([local_rows, local_carry[None]], axis=0)
    for stage in stages:
        gathered = lax.all_gather(gathered, stage, axis=2, tiled=True)
    full_rows, full_carry = gathered[:2], gathered[2]
    tokens = local_rows.shape[1]
    width = full_rows.shape[2]
    head = weights.shape[3]
    w_query = weights[0, 0]
    w_out = weights[0, 1]

    def encode():
        flat = full_rows.reshape(2 * tokens, width)
        keyval = jnp.concatenate(
            [
                jnp.dot(flat, w_query, preferred_element_type=jnp.float32),
                jnp.dot(flat, w_out, preferred_element_type=jnp.float32),
            ],
            axis=-1,
        ).astype(jnp.bfloat16)
        return (keyval, jnp.zeros((2 * tokens, head), jnp.bfloat16))

    def decode():
        queries = jnp.dot(
            full_rows.reshape(2 * tokens, width), w_query, preferred_element_type=jnp.float32
        ).astype(jnp.bfloat16)
        return (jnp.zeros((2 * tokens, 2 * head), jnp.bfloat16), queries)

    encoded, queries = lax.cond(is_encoder, encode, decode)
    per_encoder = 2 * tokens // NBLEN
    pool_blocks = encoders * per_encoder
    collected = lax.all_gather(encoded, "segment", axis=0, tiled=True)
    pool = collected[first_encoder * 2 * tokens :].reshape(pool_blocks, NBLEN, 2 * head)
    groups = tokens // GROUP
    local_nbr = neighbours[0]
    score_scale = 1.0 / math.sqrt(head)
    query_blocks = queries.reshape(2, groups, GROUP, head)

    def fetch(batch):
        picked = pool[local_nbr[batch]].reshape(groups, NEIGH * NBLEN, 2 * head)
        return (picked[..., :head], picked[..., head:])

    keys_fwd, values_fwd = fetch(0)
    soft_fwd, rounded_fwd = attend(query_blocks[0], keys_fwd, score_scale)
    mixed = jnp.einsum(
        "cqk,ckd->cqd", rounded_fwd, values_fwd, preferred_element_type=jnp.float32
    ).astype(jnp.bfloat16)
    mixed_flat = mixed.reshape(tokens, head)
    upstream = (
        jnp.dot(full_carry, w_out, preferred_element_type=jnp.float32)
        .astype(jnp.bfloat16)
        .reshape(groups, GROUP, head)
    )
    keys_back, values_back = fetch(1)
    soft_back, rounded_back = attend(query_blocks[1], keys_back, score_scale)
    grad_queries, grad_keys, grad_values = attend_back(
        query_blocks[1], keys_back, values_back, soft_back, rounded_back, upstream, score_scale
    )
    grad_flat = grad_queries.reshape(tokens, head)
    terms = jnp.stack(
        [
            lax.dot_general(w_out, mixed_flat, (((1,), (1,)), ((), ())), preferred_element_type=jnp.float32),
            lax.dot_general(w_query, grad_flat, (((1,), (1,)), ((), ())), preferred_element_type=jnp.float32),
        ]
    )
    out_sum, grad_input = head_sum(terms, mp)
    forward_rows = (local_rows[0].astype(jnp.float32) + out_sum).astype(jnp.bfloat16)
    forward_rows = jnp.where(is_encoder, local_carry, forward_rows)
    passed = from_behind(forward_rows[None], "segment", 1)
    back = local_carry.astype(jnp.float32) + grad_input
    back_rows = jnp.where(is_encoder, local_carry, back.astype(jnp.bfloat16))
    returned = from_behind(back_rows[None], "segment", -1)
    onehot = (
        local_nbr[1][..., None] == jnp.arange(pool_blocks, dtype=jnp.int32)[None, None, :]
    ).astype(jnp.float32)
    grad_keyval = jnp.concatenate([grad_keys, grad_values], axis=-1).reshape(
        groups, NEIGH, NBLEN, 2 * head
    )
    contrib = jnp.einsum("cbp,cbrf->prf", onehot, grad_keyval)
    contrib = jnp.where(is_encoder, jnp.zeros_like(contrib), contrib)
    pooled = segment_sum(contrib.astype(jnp.bfloat16).reshape(pool_blocks * NBLEN, 2 * head), "segment")
    kv_grad = pooled.reshape(pool_blocks * NBLEN, 2, head)
    return (passed, returned, kv_grad)


def split_mp(mesh):
    devices = mesh.devices
    try:
        xs = [d.coords[0] for d in devices[0]]
        ys = [d.coords[1] for d in devices[0]]
    except (AttributeError, TypeError, IndexError):
        return None
    wide = len(set(xs))
    tall = devices.shape[1] // wide
    if wide * tall != devices.shape[1] or wide == 1 or tall == 1:
        return None
    grid_x = np.array(xs).reshape(tall, wide)
    grid_y = np.array(ys).reshape(tall, wide)
    if not ((grid_x == grid_x[:1]).all() and (grid_y == grid_y[:, :1]).all()):
        return None
    return Mesh(devices.reshape(devices.shape[0], tall, wide), ("segment", "my", "mx"))


def solution(mesh):
    split = split_mp(mesh)
    if split is None:
        inner, mp, stages = mesh, "mp", ("mp",)
    else:
        inner, mp, stages = split, ("my", "mx"), ("mx", "my")
    placed = (
        P("segment", None, None, mp),
        P("segment", None, mp),
        P("segment", None, None, mp),
        P("segment", None, None, None),
    )
    return jax.shard_map(
        functools.partial(per_device, mp, stages),
        mesh=inner,
        in_specs=placed,
        out_specs=(P("segment", None, mp), P("segment", None, mp), P(None, None, mp)),
        check_vma=False,
    )
```

```python
import functools
import math

import numpy as np

import jax
import jax.numpy as jnp
from jax import lax
from jax.sharding import Mesh, PartitionSpec as P

GROUP = 64
NBLEN = 128
NEIGH = 2


def from_behind(x, axis, by):
    devices = lax.axis_size(axis)
    return lax.ppermute(x, axis, [(i, (i + by) % devices) for i in range(devices)])


def attend(queries, key_rows, score_scale):
    scores = (
        jnp.einsum("cqd,ckd->cqk", queries, key_rows, preferred_element_type=jnp.float32)
        * score_scale
    )
    soft = jax.nn.softmax(scores, axis=-1)
    return (soft, soft.astype(jnp.bfloat16))


def attend_back(queries, key_rows, value_rows, soft, rounded, upstream, score_scale):
    d_soft = jnp.einsum("cqd,ckd->cqk", upstream, value_rows, preferred_element_type=jnp.float32)
    grad_values = jnp.einsum("cqk,cqd->ckd", rounded, upstream, preferred_element_type=jnp.float32)
    d_scores = soft * (d_soft - jnp.sum(d_soft * soft, axis=-1, keepdims=True))
    grad_queries = (
        jnp.einsum("cqk,ckd->cqd", d_scores, key_rows.astype(jnp.float32)) * score_scale
    ).astype(jnp.bfloat16)
    grad_keys = jnp.einsum("cqk,cqd->ckd", d_scores, queries.astype(jnp.float32)) * score_scale
    return (grad_queries, grad_keys, grad_values)


def head_sum(terms, axis):
    devices = lax.axis_size(axis)
    count, width, tokens = terms.shape
    parts = terms.astype(jnp.bfloat16).reshape(count, devices, width // devices, tokens).transpose(1, 0, 2, 3)
    moved = lax.all_to_all(parts, axis, 0, 0, tiled=True)
    return jnp.sum(moved.astype(jnp.float32), axis=0).transpose(0, 2, 1)


def segment_sum(contrib, axis):
    devices = lax.axis_size(axis)
    parts = contrib.reshape(devices, contrib.shape[0] // devices, contrib.shape[1])
    moved = lax.all_to_all(parts, axis, 0, 0, tiled=True)
    summed = jnp.sum(moved.astype(jnp.float32), axis=0).astype(jnp.bfloat16)
    spread = jnp.broadcast_to(summed[None], (devices,) + summed.shape)
    return lax.all_to_all(spread, axis, 0, 0, tiled=True).reshape(contrib.shape)


def per_device(mp, stages, rows, carry, weights, neighbours):
    seg = ("sg", "sr")
    segments = lax.axis_size(seg)
    encoders = lax.axis_size("sr")
    first_encoder = segments - encoders
    last_group = lax.axis_size("sg") - 1
    group = lax.axis_index("sg")
    is_encoder = group == last_group
    local_rows = rows[0]
    local_carry = carry[0]
    gathered = jnp.concatenate([local_rows, local_carry[None]], axis=0)
    for stage in stages:
        gathered = lax.all_gather(gathered, stage, axis=2, tiled=True)
    full_rows, full_carry = gathered[:2], gathered[2]
    tokens = local_rows.shape[1]
    width = full_rows.shape[2]
    head = weights.shape[3]
    w_query = weights[0, 0]
    w_out = weights[0, 1]

    def encode():
        flat = full_rows.reshape(2 * tokens, width)
        keyval = jnp.concatenate(
            [
                jnp.dot(flat, w_query, preferred_element_type=jnp.float32),
                jnp.dot(flat, w_out, preferred_element_type=jnp.float32),
            ],
            axis=-1,
        ).astype(jnp.bfloat16)
        return (keyval, jnp.zeros((2 * tokens, head), jnp.bfloat16))

    def decode():
        queries = jnp.dot(
            full_rows.reshape(2 * tokens, width), w_query, preferred_element_type=jnp.float32
        ).astype(jnp.bfloat16)
        return (jnp.zeros((2 * tokens, 2 * head), jnp.bfloat16), queries)

    encoded, queries = lax.cond(is_encoder, encode, decode)
    per_encoder = 2 * tokens // NBLEN
    pool_blocks = encoders * per_encoder
    piece = encoded
    for target in range(last_group):
        arrived = lax.ppermute(encoded, "sg", [(last_group, target)])
        piece = jnp.where(group == target, arrived, piece)
    pool = lax.all_gather(piece, "sr", axis=0, tiled=True).reshape(pool_blocks, NBLEN, 2 * head)
    groups = tokens // GROUP
    local_nbr = neighbours[0]
    score_scale = 1.0 / math.sqrt(head)
    query_blocks = queries.reshape(2, groups, GROUP, head)

    def fetch(batch):
        picked = pool[local_nbr[batch]].reshape(groups, NEIGH * NBLEN, 2 * head)
        return (picked[..., :head], picked[..., head:])

    keys_fwd, values_fwd = fetch(0)
    soft_fwd, rounded_fwd = attend(query_blocks[0], keys_fwd, score_scale)
    mixed = jnp.einsum(
        "cqk,ckd->cqd", rounded_fwd, values_fwd, preferred_element_type=jnp.float32
    ).astype(jnp.bfloat16)
    mixed_flat = mixed.reshape(tokens, head)
    upstream = (
        jnp.dot(full_carry, w_out, preferred_element_type=jnp.float32)
        .astype(jnp.bfloat16)
        .reshape(groups, GROUP, head)
    )
    keys_back, values_back = fetch(1)
    soft_back, rounded_back = attend(query_blocks[1], keys_back, score_scale)
    grad_queries, grad_keys, grad_values = attend_back(
        query_blocks[1], keys_back, values_back, soft_back, rounded_back, upstream, score_scale
    )
    grad_flat = grad_queries.reshape(tokens, head)
    terms = jnp.stack(
        [
            lax.dot_general(w_out, mixed_flat, (((1,), (1,)), ((), ())), preferred_element_type=jnp.float32),
            lax.dot_general(w_query, grad_flat, (((1,), (1,)), ((), ())), preferred_element_type=jnp.float32),
        ]
    )
    out_sum, grad_input = head_sum(terms, mp)
    forward_rows = (local_rows[0].astype(jnp.float32) + out_sum).astype(jnp.bfloat16)
    forward_rows = jnp.where(is_encoder, local_carry, forward_rows)
    passed = from_behind(forward_rows[None], seg, 1)
    back = local_carry.astype(jnp.float32) + grad_input
    back_rows = jnp.where(is_encoder, local_carry, back.astype(jnp.bfloat16))
    returned = from_behind(back_rows[None], seg, -1)
    onehot = (
        local_nbr[1][..., None] == jnp.arange(pool_blocks, dtype=jnp.int32)[None, None, :]
    ).astype(jnp.float32)
    grad_keyval = jnp.concatenate([grad_keys, grad_values], axis=-1).reshape(
        groups, NEIGH, NBLEN, 2 * head
    )
    contrib = jnp.einsum("cbp,cbrf->prf", onehot, grad_keyval)
    contrib = jnp.where(is_encoder, jnp.zeros_like(contrib), contrib)
    pooled = segment_sum(contrib.astype(jnp.bfloat16).reshape(pool_blocks * NBLEN, 2 * head), seg)
    kv_grad = pooled.reshape(pool_blocks * NBLEN, 2, head)
    return (passed, returned, kv_grad)


def split_mesh(mesh):
    devices = mesh.devices
    segments = devices.shape[0]
    encoders = segments // 4
    groups = segments // encoders
    try:
        xs = [d.coords[0] for d in devices[0]]
        ys = [d.coords[1] for d in devices[0]]
        wide = len(set(xs))
        tall = devices.shape[1] // wide
        grid_x = np.array(xs).reshape(tall, wide)
        grid_y = np.array(ys).reshape(tall, wide)
        ok = (
            wide * tall == devices.shape[1]
            and wide > 1
            and tall > 1
            and (grid_x == grid_x[:1]).all()
            and (grid_y == grid_y[:, :1]).all()
        )
    except (AttributeError, TypeError, IndexError, ValueError):
        ok = False
    if ok:
        view = devices.reshape(groups, encoders, tall, wide)
        return Mesh(view, ("sg", "sr", "my", "mx")), ("my", "mx"), ("mx", "my")
    view = devices.reshape(groups, encoders, devices.shape[1])
    return Mesh(view, ("sg", "sr", "mp")), "mp", ("mp",)


def solution(mesh):
    inner, mp, stages = split_mesh(mesh)
    seg = ("sg", "sr")
    placed = (
        P(seg, None, None, mp),
        P(seg, None, mp),
        P(seg, None, None, mp),
        P(seg, None, None, None),
    )
    return jax.shard_map(
        functools.partial(per_device, mp, stages),
        mesh=inner,
        in_specs=placed,
        out_specs=(P(seg, None, mp), P(seg, None, mp), P(None, None, mp)),
        check_vma=False,
    )
```

```python
import functools
import math

import numpy as np

import jax
import jax.numpy as jnp
from jax import lax
from jax.sharding import Mesh, PartitionSpec as P

GROUP = 64
NBLEN = 128
NEIGH = 2


def from_behind(x, axis, by):
    devices = lax.axis_size(axis)
    return lax.ppermute(x, axis, [(i, (i + by) % devices) for i in range(devices)])


def attend(queries, key_rows, score_scale):
    scores = (
        jnp.einsum("cqd,ckd->cqk", queries, key_rows, preferred_element_type=jnp.float32)
        * score_scale
    )
    soft = jax.nn.softmax(scores, axis=-1)
    return (soft, soft.astype(jnp.bfloat16))


def attend_back(queries, key_rows, value_rows, soft, rounded, upstream, score_scale):
    d_soft = jnp.einsum("cqd,ckd->cqk", upstream, value_rows, preferred_element_type=jnp.float32)
    grad_values = jnp.einsum("cqk,cqd->ckd", rounded, upstream, preferred_element_type=jnp.float32)
    d_scores = soft * (d_soft - jnp.sum(d_soft * soft, axis=-1, keepdims=True))
    grad_queries = (
        jnp.einsum("cqk,ckd->cqd", d_scores, key_rows.astype(jnp.float32)) * score_scale
    ).astype(jnp.bfloat16)
    grad_keys = jnp.einsum("cqk,cqd->ckd", d_scores, queries.astype(jnp.float32)) * score_scale
    return (grad_queries, grad_keys, grad_values)


def ring_sum(chunks, axis):
    n = chunks.shape[0]
    me = lax.axis_index(axis)
    half = chunks.shape[-1] // 2
    ahead, behind = chunks[..., :half], chunks[..., half:]

    def take(part, offset):
        return lax.dynamic_index_in_dim(part, (me + offset) % n, 0, keepdims=False)

    up, down = take(ahead, n - 1), take(behind, 1)
    for step in range(n - 1):
        up = lax.ppermute(up, axis, [(i, (i + 1) % n) for i in range(n)])
        down = lax.ppermute(down, axis, [(i, (i - 1) % n) for i in range(n)])
        up = up + take(ahead, 2 * n - 2 - step)
        down = down + take(behind, 2 + step)
    return jnp.concatenate([up, down], axis=-1)


def head_sum(terms, axis):
    count, width, tokens = terms.shape
    rounded = terms.astype(jnp.bfloat16)
    if isinstance(axis, tuple):
        tall, wide = lax.axis_size(axis[0]), lax.axis_size(axis[1])
        parts = rounded.reshape(count, tall, wide, width // (tall * wide), tokens).transpose(2, 1, 0, 3, 4)
        moved = lax.all_to_all(parts, axis[1], 0, 0, tiled=True)
        partial = jnp.sum(moved.astype(jnp.float32), axis=0)
        summed = ring_sum(partial, axis[0])
    else:
        devices = lax.axis_size(axis)
        parts = rounded.reshape(count, devices, width // devices, tokens).transpose(1, 0, 2, 3)
        moved = lax.all_to_all(parts, axis, 0, 0, tiled=True)
        summed = jnp.sum(moved.astype(jnp.float32), axis=0)
    return summed.transpose(0, 2, 1)


def segment_sum(contrib, axis):
    devices = lax.axis_size(axis)
    parts = contrib.reshape(devices, contrib.shape[0] // devices, contrib.shape[1])
    moved = lax.all_to_all(parts, axis, 0, 0, tiled=True)
    summed = jnp.sum(moved.astype(jnp.float32), axis=0).astype(jnp.bfloat16)
    spread = jnp.broadcast_to(summed[None], (devices,) + summed.shape)
    return lax.all_to_all(spread, axis, 0, 0, tiled=True).reshape(contrib.shape)


def per_device(mp, stages, rows, carry, weights, neighbours):
    seg = ("sg", "sr")
    segments = lax.axis_size(seg)
    encoders = lax.axis_size("sr")
    first_encoder = segments - encoders
    last_group = lax.axis_size("sg") - 1
    group = lax.axis_index("sg")
    is_encoder = group == last_group
    local_rows = rows[0]
    local_carry = carry[0]
    gathered = jnp.concatenate([local_rows, local_carry[None]], axis=0)
    for stage in stages:
        gathered = lax.all_gather(gathered, stage, axis=2, tiled=True)
    full_rows, full_carry = gathered[:2], gathered[2]
    tokens = local_rows.shape[1]
    width = full_rows.shape[2]
    head = weights.shape[3]
    w_query = weights[0, 0]
    w_out = weights[0, 1]

    def encode():
        flat = full_rows.reshape(2 * tokens, width)
        keyval = jnp.concatenate(
            [
                jnp.dot(flat, w_query, preferred_element_type=jnp.float32),
                jnp.dot(flat, w_out, preferred_element_type=jnp.float32),
            ],
            axis=-1,
        ).astype(jnp.bfloat16)
        return (keyval, jnp.zeros((2 * tokens, head), jnp.bfloat16))

    def decode():
        queries = jnp.dot(
            full_rows.reshape(2 * tokens, width), w_query, preferred_element_type=jnp.float32
        ).astype(jnp.bfloat16)
        return (jnp.zeros((2 * tokens, 2 * head), jnp.bfloat16), queries)

    encoded, queries = lax.cond(is_encoder, encode, decode)
    per_encoder = 2 * tokens // NBLEN
    pool_blocks = encoders * per_encoder
    piece = encoded
    for target in range(last_group):
        arrived = lax.ppermute(encoded, "sg", [(last_group, target)])
        piece = jnp.where(group == target, arrived, piece)
    pool = lax.all_gather(piece, "sr", axis=0, tiled=True).reshape(pool_blocks, NBLEN, 2 * head)
    groups = tokens // GROUP
    local_nbr = neighbours[0]
    score_scale = 1.0 / math.sqrt(head)
    query_blocks = queries.reshape(2, groups, GROUP, head)

    def fetch(batch):
        picked = pool[local_nbr[batch]].reshape(groups, NEIGH * NBLEN, 2 * head)
        return (picked[..., :head], picked[..., head:])

    keys_fwd, values_fwd = fetch(0)
    soft_fwd, rounded_fwd = attend(query_blocks[0], keys_fwd, score_scale)
    mixed = jnp.einsum(
        "cqk,ckd->cqd", rounded_fwd, values_fwd, preferred_element_type=jnp.float32
    ).astype(jnp.bfloat16)
    mixed_flat = mixed.reshape(tokens, head)
    upstream = (
        jnp.dot(full_carry, w_out, preferred_element_type=jnp.float32)
        .astype(jnp.bfloat16)
        .reshape(groups, GROUP, head)
    )
    keys_back, values_back = fetch(1)
    soft_back, rounded_back = attend(query_blocks[1], keys_back, score_scale)
    grad_queries, grad_keys, grad_values = attend_back(
        query_blocks[1], keys_back, values_back, soft_back, rounded_back, upstream, score_scale
    )
    grad_flat = grad_queries.reshape(tokens, head)
    terms = jnp.stack(
        [
            lax.dot_general(w_out, mixed_flat, (((1,), (1,)), ((), ())), preferred_element_type=jnp.float32),
            lax.dot_general(w_query, grad_flat, (((1,), (1,)), ((), ())), preferred_element_type=jnp.float32),
        ]
    )
    out_sum, grad_input = head_sum(terms, mp)
    forward_rows = (local_rows[0].astype(jnp.float32) + out_sum).astype(jnp.bfloat16)
    forward_rows = jnp.where(is_encoder, local_carry, forward_rows)
    passed = from_behind(forward_rows[None], seg, 1)
    back = local_carry.astype(jnp.float32) + grad_input
    back_rows = jnp.where(is_encoder, local_carry, back.astype(jnp.bfloat16))
    returned = from_behind(back_rows[None], seg, -1)
    onehot = (
        local_nbr[1][..., None] == jnp.arange(pool_blocks, dtype=jnp.int32)[None, None, :]
    ).astype(jnp.float32)
    grad_keyval = jnp.concatenate([grad_keys, grad_values], axis=-1).reshape(
        groups, NEIGH, NBLEN, 2 * head
    )
    contrib = jnp.einsum("cbp,cbrf->prf", onehot, grad_keyval)
    contrib = jnp.where(is_encoder, jnp.zeros_like(contrib), contrib)
    pooled = segment_sum(contrib.astype(jnp.bfloat16).reshape(pool_blocks * NBLEN, 2 * head), seg)
    kv_grad = pooled.reshape(pool_blocks * NBLEN, 2, head)
    return (passed, returned, kv_grad)


def split_mesh(mesh):
    devices = mesh.devices
    segments = devices.shape[0]
    encoders = segments // 4
    groups = segments // encoders
    try:
        xs = [d.coords[0] for d in devices[0]]
        ys = [d.coords[1] for d in devices[0]]
        wide = len(set(xs))
        tall = devices.shape[1] // wide
        grid_x = np.array(xs).reshape(tall, wide)
        grid_y = np.array(ys).reshape(tall, wide)
        ok = (
            wide * tall == devices.shape[1]
            and wide > 1
            and tall > 1
            and (grid_x == grid_x[:1]).all()
            and (grid_y == grid_y[:, :1]).all()
        )
    except (AttributeError, TypeError, IndexError, ValueError):
        ok = False
    if ok:
        view = devices.reshape(groups, encoders, tall, wide)
        return Mesh(view, ("sg", "sr", "my", "mx")), ("my", "mx"), ("mx", "my")
    view = devices.reshape(groups, encoders, devices.shape[1])
    return Mesh(view, ("sg", "sr", "mp")), "mp", ("mp",)


def solution(mesh):
    inner, mp, stages = split_mesh(mesh)
    seg = ("sg", "sr")
    placed = (
        P(seg, None, None, mp),
        P(seg, None, mp),
        P(seg, None, None, mp),
        P(seg, None, None, None),
    )
    return jax.shard_map(
        functools.partial(per_device, mp, stages),
        mesh=inner,
        in_specs=placed,
        out_specs=(P(seg, None, mp), P(seg, None, mp), P(None, None, mp)),
        check_vma=False,
    )
```

```python
import functools
import math

import numpy as np

import jax
import jax.numpy as jnp
from jax import lax
from jax.sharding import Mesh, PartitionSpec as P

GROUP = 64
NBLEN = 128
NEIGH = 2


def from_behind(x, axis, by):
    devices = lax.axis_size(axis)
    return lax.ppermute(x, axis, [(i, (i + by) % devices) for i in range(devices)])


def attend(queries, key_rows, score_scale):
    scores = (
        jnp.einsum("cqd,ckd->cqk", queries, key_rows, preferred_element_type=jnp.float32)
        * score_scale
    )
    soft = jax.nn.softmax(scores, axis=-1)
    return (soft, soft.astype(jnp.bfloat16))


def attend_back(queries, key_rows, value_rows, soft, rounded, upstream, score_scale):
    d_soft = jnp.einsum("cqd,ckd->cqk", upstream, value_rows, preferred_element_type=jnp.float32)
    grad_values = jnp.einsum("cqk,cqd->ckd", rounded, upstream, preferred_element_type=jnp.float32)
    d_scores = soft * (d_soft - jnp.sum(d_soft * soft, axis=-1, keepdims=True))
    grad_queries = (
        jnp.einsum("cqk,ckd->cqd", d_scores, key_rows.astype(jnp.float32)) * score_scale
    ).astype(jnp.bfloat16)
    grad_keys = jnp.einsum("cqk,cqd->ckd", d_scores, queries.astype(jnp.float32)) * score_scale
    return (grad_queries, grad_keys, grad_values)


def ring_sum(chunks, axis):
    n = chunks.shape[0]
    me = lax.axis_index(axis)
    half = chunks.shape[-1] // 2
    ahead, behind = chunks[..., :half], chunks[..., half:]

    def take(part, offset):
        return lax.dynamic_index_in_dim(part, (me + offset) % n, 0, keepdims=False).astype(jnp.float32)

    up, down = take(ahead, n - 1), take(behind, 1)
    for step in range(n - 1):
        up = lax.ppermute(up.astype(jnp.bfloat16), axis, [(i, (i + 1) % n) for i in range(n)])
        down = lax.ppermute(down.astype(jnp.bfloat16), axis, [(i, (i - 1) % n) for i in range(n)])
        up = up.astype(jnp.float32) + take(ahead, 2 * n - 2 - step)
        down = down.astype(jnp.float32) + take(behind, 2 + step)
    return jnp.concatenate([up, down], axis=-1)


def head_sum(terms, axis):
    count, width, tokens = terms.shape
    rounded = terms.astype(jnp.bfloat16)
    if isinstance(axis, tuple):
        tall, wide = lax.axis_size(axis[0]), lax.axis_size(axis[1])
        parts = rounded.reshape(count, tall, wide, width // (tall * wide), tokens).transpose(1, 2, 0, 3, 4)
        partial = ring_sum(parts, axis[0])
        moved = lax.all_to_all(partial, axis[1], 0, 0, tiled=True)
        summed = jnp.sum(moved, axis=0)
    else:
        devices = lax.axis_size(axis)
        parts = rounded.reshape(count, devices, width // devices, tokens).transpose(1, 0, 2, 3)
        moved = lax.all_to_all(parts, axis, 0, 0, tiled=True)
        summed = jnp.sum(moved.astype(jnp.float32), axis=0)
    return summed.transpose(0, 2, 1)


def segment_sum(contrib, axis):
    devices = lax.axis_size(axis)
    parts = contrib.reshape(devices, contrib.shape[0] // devices, contrib.shape[1])
    moved = lax.all_to_all(parts, axis, 0, 0, tiled=True)
    summed = jnp.sum(moved.astype(jnp.float32), axis=0).astype(jnp.bfloat16)
    spread = jnp.broadcast_to(summed[None], (devices,) + summed.shape)
    return lax.all_to_all(spread, axis, 0, 0, tiled=True).reshape(contrib.shape)


def per_device(mp, stages, rows, carry, weights, neighbours):
    seg = ("sg", "sr")
    segments = lax.axis_size(seg)
    encoders = lax.axis_size("sr")
    first_encoder = segments - encoders
    last_group = lax.axis_size("sg") - 1
    group = lax.axis_index("sg")
    is_encoder = group == last_group
    local_rows = rows[0]
    local_carry = carry[0]
    gathered = jnp.concatenate([local_rows, local_carry[None]], axis=0)
    for stage in stages:
        gathered = lax.all_gather(gathered, stage, axis=2, tiled=True)
    full_rows, full_carry = gathered[:2], gathered[2]
    tokens = local_rows.shape[1]
    width = full_rows.shape[2]
    head = weights.shape[3]
    w_query = weights[0, 0]
    w_out = weights[0, 1]

    def encode():
        flat = full_rows.reshape(2 * tokens, width)
        keyval = jnp.concatenate(
            [
                jnp.dot(flat, w_query, preferred_element_type=jnp.float32),
                jnp.dot(flat, w_out, preferred_element_type=jnp.float32),
            ],
            axis=-1,
        ).astype(jnp.bfloat16)
        return (keyval, jnp.zeros((2 * tokens, head), jnp.bfloat16))

    def decode():
        queries = jnp.dot(
            full_rows.reshape(2 * tokens, width), w_query, preferred_element_type=jnp.float32
        ).astype(jnp.bfloat16)
        return (jnp.zeros((2 * tokens, 2 * head), jnp.bfloat16), queries)

    encoded, queries = lax.cond(is_encoder, encode, decode)
    per_encoder = 2 * tokens // NBLEN
    pool_blocks = encoders * per_encoder
    piece = encoded
    for target in range(last_group):
        arrived = lax.ppermute(encoded, "sg", [(last_group, target)])
        piece = jnp.where(group == target, arrived, piece)
    pool = lax.all_gather(piece, "sr", axis=0, tiled=True).reshape(pool_blocks, NBLEN, 2 * head)
    groups = tokens // GROUP
    local_nbr = neighbours[0]
    score_scale = 1.0 / math.sqrt(head)
    query_blocks = queries.reshape(2, groups, GROUP, head)

    def fetch(batch):
        picked = pool[local_nbr[batch]].reshape(groups, NEIGH * NBLEN, 2 * head)
        return (picked[..., :head], picked[..., head:])

    keys_fwd, values_fwd = fetch(0)
    soft_fwd, rounded_fwd = attend(query_blocks[0], keys_fwd, score_scale)
    mixed = jnp.einsum(
        "cqk,ckd->cqd", rounded_fwd, values_fwd, preferred_element_type=jnp.float32
    ).astype(jnp.bfloat16)
    mixed_flat = mixed.reshape(tokens, head)
    upstream = (
        jnp.dot(full_carry, w_out, preferred_element_type=jnp.float32)
        .astype(jnp.bfloat16)
        .reshape(groups, GROUP, head)
    )
    keys_back, values_back = fetch(1)
    soft_back, rounded_back = attend(query_blocks[1], keys_back, score_scale)
    grad_queries, grad_keys, grad_values = attend_back(
        query_blocks[1], keys_back, values_back, soft_back, rounded_back, upstream, score_scale
    )
    grad_flat = grad_queries.reshape(tokens, head)
    terms = jnp.stack(
        [
            lax.dot_general(w_out, mixed_flat, (((1,), (1,)), ((), ())), preferred_element_type=jnp.float32),
            lax.dot_general(w_query, grad_flat, (((1,), (1,)), ((), ())), preferred_element_type=jnp.float32),
        ]
    )
    out_sum, grad_input = head_sum(terms, mp)
    forward_rows = (local_rows[0].astype(jnp.float32) + out_sum).astype(jnp.bfloat16)
    forward_rows = jnp.where(is_encoder, local_carry, forward_rows)
    passed = from_behind(forward_rows[None], seg, 1)
    back = local_carry.astype(jnp.float32) + grad_input
    back_rows = jnp.where(is_encoder, local_carry, back.astype(jnp.bfloat16))
    returned = from_behind(back_rows[None], seg, -1)
    onehot = (
        local_nbr[1][..., None] == jnp.arange(pool_blocks, dtype=jnp.int32)[None, None, :]
    ).astype(jnp.float32)
    grad_keyval = jnp.concatenate([grad_keys, grad_values], axis=-1).reshape(
        groups, NEIGH, NBLEN, 2 * head
    )
    contrib = jnp.einsum("cbp,cbrf->prf", onehot, grad_keyval)
    contrib = jnp.where(is_encoder, jnp.zeros_like(contrib), contrib)
    pooled = segment_sum(contrib.astype(jnp.bfloat16).reshape(pool_blocks * NBLEN, 2 * head), seg)
    kv_grad = pooled.reshape(pool_blocks * NBLEN, 2, head)
    return (passed, returned, kv_grad)


def split_mesh(mesh):
    devices = mesh.devices
    segments = devices.shape[0]
    encoders = segments // 4
    groups = segments // encoders
    try:
        xs = [d.coords[0] for d in devices[0]]
        ys = [d.coords[1] for d in devices[0]]
        wide = len(set(xs))
        tall = devices.shape[1] // wide
        grid_x = np.array(xs).reshape(tall, wide)
        grid_y = np.array(ys).reshape(tall, wide)
        ok = (
            wide * tall == devices.shape[1]
            and wide > 1
            and tall > 1
            and (grid_x == grid_x[:1]).all()
            and (grid_y == grid_y[:, :1]).all()
        )
    except (AttributeError, TypeError, IndexError, ValueError):
        ok = False
    if ok:
        view = devices.reshape(groups, encoders, tall, wide)
        return Mesh(view, ("sg", "sr", "my", "mx")), ("my", "mx"), ("mx", "my")
    view = devices.reshape(groups, encoders, devices.shape[1])
    return Mesh(view, ("sg", "sr", "mp")), "mp", ("mp",)


def solution(mesh):
    inner, mp, stages = split_mesh(mesh)
    seg = ("sg", "sr")
    placed = (
        P(seg, None, None, mp),
        P(seg, None, mp),
        P(seg, None, None, mp),
        P(seg, None, None, None),
    )
    return jax.shard_map(
        functools.partial(per_device, mp, stages),
        mesh=inner,
        in_specs=placed,
        out_specs=(P(seg, None, mp), P(seg, None, mp), P(None, None, mp)),
        check_vma=False,
    )
```

```python
import functools
import math

import numpy as np

import jax
import jax.numpy as jnp
from jax import lax
from jax.sharding import Mesh, PartitionSpec as P

GROUP = 64
NBLEN = 128
NEIGH = 2


def from_behind(x, axis, by):
    devices = lax.axis_size(axis)
    return lax.ppermute(x, axis, [(i, (i + by) % devices) for i in range(devices)])


def attend(queries, key_rows, score_scale):
    scores = (
        jnp.einsum("cqd,ckd->cqk", queries, key_rows, preferred_element_type=jnp.float32)
        * score_scale
    )
    soft = jax.nn.softmax(scores, axis=-1)
    return (soft, soft.astype(jnp.bfloat16))


def attend_back(queries, key_rows, value_rows, soft, rounded, upstream, score_scale):
    d_soft = jnp.einsum("cqd,ckd->cqk", upstream, value_rows, preferred_element_type=jnp.float32)
    grad_values = jnp.einsum("cqk,cqd->ckd", rounded, upstream, preferred_element_type=jnp.float32)
    d_scores = soft * (d_soft - jnp.sum(d_soft * soft, axis=-1, keepdims=True))
    grad_queries = (
        jnp.einsum("cqk,ckd->cqd", d_scores, key_rows.astype(jnp.float32)) * score_scale
    ).astype(jnp.bfloat16)
    grad_keys = jnp.einsum("cqk,cqd->ckd", d_scores, queries.astype(jnp.float32)) * score_scale
    return (grad_queries, grad_keys, grad_values)


def head_sum(terms, axis):
    count, width, tokens = terms.shape
    rounded = terms.astype(jnp.bfloat16)
    if isinstance(axis, tuple):
        tall, wide = lax.axis_size(axis[0]), lax.axis_size(axis[1])
        parts = rounded.reshape(count, tall, wide, width // (tall * wide), tokens).transpose(1, 2, 0, 3, 4)
        partial = lax.psum_scatter(parts, axis[0], scatter_dimension=0, tiled=True)[0]
        moved = lax.all_to_all(partial.astype(jnp.float32), axis[1], 0, 0, tiled=True)
        summed = jnp.sum(moved, axis=0)
    else:
        devices = lax.axis_size(axis)
        parts = rounded.reshape(count, devices, width // devices, tokens).transpose(1, 0, 2, 3)
        moved = lax.all_to_all(parts, axis, 0, 0, tiled=True)
        summed = jnp.sum(moved.astype(jnp.float32), axis=0)
    return summed.transpose(0, 2, 1)


def segment_sum(contrib, axis):
    devices = lax.axis_size(axis)
    parts = contrib.reshape(devices, contrib.shape[0] // devices, contrib.shape[1])
    moved = lax.all_to_all(parts, axis, 0, 0, tiled=True)
    summed = jnp.sum(moved.astype(jnp.float32), axis=0).astype(jnp.bfloat16)
    spread = jnp.broadcast_to(summed[None], (devices,) + summed.shape)
    return lax.all_to_all(spread, axis, 0, 0, tiled=True).reshape(contrib.shape)


def per_device(mp, stages, rows, carry, weights, neighbours):
    seg = ("sg", "sr")
    segments = lax.axis_size(seg)
    encoders = lax.axis_size("sr")
    first_encoder = segments - encoders
    last_group = lax.axis_size("sg") - 1
    group = lax.axis_index("sg")
    is_encoder = group == last_group
    local_rows = rows[0]
    local_carry = carry[0]
    gathered = jnp.concatenate([local_rows, local_carry[None]], axis=0)
    for stage in stages:
        gathered = lax.all_gather(gathered, stage, axis=2, tiled=True)
    full_rows, full_carry = gathered[:2], gathered[2]
    tokens = local_rows.shape[1]
    width = full_rows.shape[2]
    head = weights.shape[3]
    w_query = weights[0, 0]
    w_out = weights[0, 1]

    def encode():
        flat = full_rows.reshape(2 * tokens, width)
        keyval = jnp.concatenate(
            [
                jnp.dot(flat, w_query, preferred_element_type=jnp.float32),
                jnp.dot(flat, w_out, preferred_element_type=jnp.float32),
            ],
            axis=-1,
        ).astype(jnp.bfloat16)
        return (keyval, jnp.zeros((2 * tokens, head), jnp.bfloat16))

    def decode():
        queries = jnp.dot(
            full_rows.reshape(2 * tokens, width), w_query, preferred_element_type=jnp.float32
        ).astype(jnp.bfloat16)
        return (jnp.zeros((2 * tokens, 2 * head), jnp.bfloat16), queries)

    encoded, queries = lax.cond(is_encoder, encode, decode)
    per_encoder = 2 * tokens // NBLEN
    pool_blocks = encoders * per_encoder
    piece = encoded
    for target in range(last_group):
        arrived = lax.ppermute(encoded, "sg", [(last_group, target)])
        piece = jnp.where(group == target, arrived, piece)
    pool = lax.all_gather(piece, "sr", axis=0, tiled=True).reshape(pool_blocks, NBLEN, 2 * head)
    groups = tokens // GROUP
    local_nbr = neighbours[0]
    score_scale = 1.0 / math.sqrt(head)
    query_blocks = queries.reshape(2, groups, GROUP, head)

    def fetch(batch):
        picked = pool[local_nbr[batch]].reshape(groups, NEIGH * NBLEN, 2 * head)
        return (picked[..., :head], picked[..., head:])

    keys_fwd, values_fwd = fetch(0)
    soft_fwd, rounded_fwd = attend(query_blocks[0], keys_fwd, score_scale)
    mixed = jnp.einsum(
        "cqk,ckd->cqd", rounded_fwd, values_fwd, preferred_element_type=jnp.float32
    ).astype(jnp.bfloat16)
    mixed_flat = mixed.reshape(tokens, head)
    upstream = (
        jnp.dot(full_carry, w_out, preferred_element_type=jnp.float32)
        .astype(jnp.bfloat16)
        .reshape(groups, GROUP, head)
    )
    keys_back, values_back = fetch(1)
    soft_back, rounded_back = attend(query_blocks[1], keys_back, score_scale)
    grad_queries, grad_keys, grad_values = attend_back(
        query_blocks[1], keys_back, values_back, soft_back, rounded_back, upstream, score_scale
    )
    grad_flat = grad_queries.reshape(tokens, head)
    terms = jnp.stack(
        [
            lax.dot_general(w_out, mixed_flat, (((1,), (1,)), ((), ())), preferred_element_type=jnp.float32),
            lax.dot_general(w_query, grad_flat, (((1,), (1,)), ((), ())), preferred_element_type=jnp.float32),
        ]
    )
    out_sum, grad_input = head_sum(terms, mp)
    forward_rows = (local_rows[0].astype(jnp.float32) + out_sum).astype(jnp.bfloat16)
    forward_rows = jnp.where(is_encoder, local_carry, forward_rows)
    passed = from_behind(forward_rows[None], seg, 1)
    back = local_carry.astype(jnp.float32) + grad_input
    back_rows = jnp.where(is_encoder, local_carry, back.astype(jnp.bfloat16))
    returned = from_behind(back_rows[None], seg, -1)
    onehot = (
        local_nbr[1][..., None] == jnp.arange(pool_blocks, dtype=jnp.int32)[None, None, :]
    ).astype(jnp.float32)
    grad_keyval = jnp.concatenate([grad_keys, grad_values], axis=-1).reshape(
        groups, NEIGH, NBLEN, 2 * head
    )
    contrib = jnp.einsum("cbp,cbrf->prf", onehot, grad_keyval)
    contrib = jnp.where(is_encoder, jnp.zeros_like(contrib), contrib)
    pooled = segment_sum(contrib.astype(jnp.bfloat16).reshape(pool_blocks * NBLEN, 2 * head), seg)
    kv_grad = pooled.reshape(pool_blocks * NBLEN, 2, head)
    return (passed, returned, kv_grad)


def split_mesh(mesh):
    devices = mesh.devices
    segments = devices.shape[0]
    encoders = segments // 4
    groups = segments // encoders
    try:
        xs = [d.coords[0] for d in devices[0]]
        ys = [d.coords[1] for d in devices[0]]
        wide = len(set(xs))
        tall = devices.shape[1] // wide
        grid_x = np.array(xs).reshape(tall, wide)
        grid_y = np.array(ys).reshape(tall, wide)
        ok = (
            wide * tall == devices.shape[1]
            and wide > 1
            and tall > 1
            and (grid_x == grid_x[:1]).all()
            and (grid_y == grid_y[:, :1]).all()
        )
    except (AttributeError, TypeError, IndexError, ValueError):
        ok = False
    if ok:
        view = devices.reshape(groups, encoders, tall, wide)
        return Mesh(view, ("sg", "sr", "my", "mx")), ("my", "mx"), ("mx", "my")
    view = devices.reshape(groups, encoders, devices.shape[1])
    return Mesh(view, ("sg", "sr", "mp")), "mp", ("mp",)


def solution(mesh):
    inner, mp, stages = split_mesh(mesh)
    seg = ("sg", "sr")
    placed = (
        P(seg, None, None, mp),
        P(seg, None, mp),
        P(seg, None, None, mp),
        P(seg, None, None, None),
    )
    return jax.shard_map(
        functools.partial(per_device, mp, stages),
        mesh=inner,
        in_specs=placed,
        out_specs=(P(seg, None, mp), P(seg, None, mp), P(None, None, mp)),
        check_vma=False,
    )
```

```python
import functools
import math

import numpy as np

import jax
import jax.numpy as jnp
from jax import lax
from jax.sharding import Mesh, PartitionSpec as P

GROUP = 64
NBLEN = 128
NEIGH = 2


def from_behind(x, axis, by):
    devices = lax.axis_size(axis)
    return lax.ppermute(x, axis, [(i, (i + by) % devices) for i in range(devices)])


def attend(queries, key_rows, score_scale):
    scores = (
        jnp.einsum("cqd,ckd->cqk", queries, key_rows, preferred_element_type=jnp.float32)
        * score_scale
    )
    soft = jax.nn.softmax(scores, axis=-1)
    return (soft, soft.astype(jnp.bfloat16))


def attend_back(queries, key_rows, value_rows, soft, rounded, upstream, score_scale):
    d_soft = jnp.einsum("cqd,ckd->cqk", upstream, value_rows, preferred_element_type=jnp.float32)
    grad_values = jnp.einsum("cqk,cqd->ckd", rounded, upstream, preferred_element_type=jnp.float32)
    d_scores = soft * (d_soft - jnp.sum(d_soft * soft, axis=-1, keepdims=True))
    grad_queries = (
        jnp.einsum("cqk,ckd->cqd", d_scores, key_rows.astype(jnp.float32)) * score_scale
    ).astype(jnp.bfloat16)
    grad_keys = jnp.einsum("cqk,cqd->ckd", d_scores, queries.astype(jnp.float32)) * score_scale
    return (grad_queries, grad_keys, grad_values)


def head_sum(terms, axis, tie):
    count, width, tokens = terms.shape
    rounded = terms.astype(jnp.bfloat16)
    if isinstance(axis, tuple):
        tall, wide = lax.axis_size(axis[0]), lax.axis_size(axis[1])
        parts = rounded.reshape(count, tall, wide, width // (tall * wide), tokens).transpose(1, 2, 0, 3, 4)
        partial = lax.psum_scatter(parts, axis[0], scatter_dimension=0, tiled=True)[0]
        partial, tie = lax.optimization_barrier((partial, tie))
        moved = lax.all_to_all(partial.astype(jnp.float32), axis[1], 0, 0, tiled=True)
        summed = jnp.sum(moved, axis=0)
    else:
        devices = lax.axis_size(axis)
        parts = rounded.reshape(count, devices, width // devices, tokens).transpose(1, 0, 2, 3)
        moved = lax.all_to_all(parts, axis, 0, 0, tiled=True)
        summed = jnp.sum(moved.astype(jnp.float32), axis=0)
    return summed.transpose(0, 2, 1), tie


def segment_sum(contrib, axis):
    devices = lax.axis_size(axis)
    parts = contrib.reshape(devices, contrib.shape[0] // devices, contrib.shape[1])
    moved = lax.all_to_all(parts, axis, 0, 0, tiled=True)
    summed = jnp.sum(moved.astype(jnp.float32), axis=0).astype(jnp.bfloat16)
    spread = jnp.broadcast_to(summed[None], (devices,) + summed.shape)
    return lax.all_to_all(spread, axis, 0, 0, tiled=True).reshape(contrib.shape)


def per_device(mp, stages, rows, carry, weights, neighbours):
    seg = ("sg", "sr")
    segments = lax.axis_size(seg)
    encoders = lax.axis_size("sr")
    first_encoder = segments - encoders
    last_group = lax.axis_size("sg") - 1
    group = lax.axis_index("sg")
    is_encoder = group == last_group
    local_rows = rows[0]
    local_carry = carry[0]
    gathered = jnp.concatenate([local_rows, local_carry[None]], axis=0)
    for stage in stages:
        gathered = lax.all_gather(gathered, stage, axis=2, tiled=True)
    full_rows, full_carry = gathered[:2], gathered[2]
    tokens = local_rows.shape[1]
    width = full_rows.shape[2]
    head = weights.shape[3]
    w_query = weights[0, 0]
    w_out = weights[0, 1]

    def encode():
        flat = full_rows.reshape(2 * tokens, width)
        keyval = jnp.concatenate(
            [
                jnp.dot(flat, w_query, preferred_element_type=jnp.float32),
                jnp.dot(flat, w_out, preferred_element_type=jnp.float32),
            ],
            axis=-1,
        ).astype(jnp.bfloat16)
        return (keyval, jnp.zeros((2 * tokens, head), jnp.bfloat16))

    def decode():
        queries = jnp.dot(
            full_rows.reshape(2 * tokens, width), w_query, preferred_element_type=jnp.float32
        ).astype(jnp.bfloat16)
        return (jnp.zeros((2 * tokens, 2 * head), jnp.bfloat16), queries)

    encoded, queries = lax.cond(is_encoder, encode, decode)
    per_encoder = 2 * tokens // NBLEN
    pool_blocks = encoders * per_encoder
    piece = encoded
    for target in range(last_group):
        arrived = lax.ppermute(encoded, "sg", [(last_group, target)])
        piece = jnp.where(group == target, arrived, piece)
    pool = lax.all_gather(piece, "sr", axis=0, tiled=True).reshape(pool_blocks, NBLEN, 2 * head)
    groups = tokens // GROUP
    local_nbr = neighbours[0]
    score_scale = 1.0 / math.sqrt(head)
    query_blocks = queries.reshape(2, groups, GROUP, head)

    def fetch(batch):
        picked = pool[local_nbr[batch]].reshape(groups, NEIGH * NBLEN, 2 * head)
        return (picked[..., :head], picked[..., head:])

    keys_fwd, values_fwd = fetch(0)
    soft_fwd, rounded_fwd = attend(query_blocks[0], keys_fwd, score_scale)
    mixed = jnp.einsum(
        "cqk,ckd->cqd", rounded_fwd, values_fwd, preferred_element_type=jnp.float32
    ).astype(jnp.bfloat16)
    mixed_flat = mixed.reshape(tokens, head)
    upstream = (
        jnp.dot(full_carry, w_out, preferred_element_type=jnp.float32)
        .astype(jnp.bfloat16)
        .reshape(groups, GROUP, head)
    )
    keys_back, values_back = fetch(1)
    soft_back, rounded_back = attend(query_blocks[1], keys_back, score_scale)
    grad_queries, grad_keys, grad_values = attend_back(
        query_blocks[1], keys_back, values_back, soft_back, rounded_back, upstream, score_scale
    )
    grad_flat = grad_queries.reshape(tokens, head)
    terms = jnp.stack(
        [
            lax.dot_general(w_out, mixed_flat, (((1,), (1,)), ((), ())), preferred_element_type=jnp.float32),
            lax.dot_general(w_query, grad_flat, (((1,), (1,)), ((), ())), preferred_element_type=jnp.float32),
        ]
    )
    onehot = (
        local_nbr[1][..., None] == jnp.arange(pool_blocks, dtype=jnp.int32)[None, None, :]
    ).astype(jnp.float32)
    grad_keyval = jnp.concatenate([grad_keys, grad_values], axis=-1).reshape(
        groups, NEIGH, NBLEN, 2 * head
    )
    contrib = jnp.einsum("cbp,cbrf->prf", onehot, grad_keyval)
    contrib = jnp.where(is_encoder, jnp.zeros_like(contrib), contrib)
    pooled = segment_sum(contrib.astype(jnp.bfloat16).reshape(pool_blocks * NBLEN, 2 * head), seg)
    kv_grad = pooled.reshape(pool_blocks * NBLEN, 2, head)
    summed, kv_grad = head_sum(terms, mp, kv_grad)
    out_sum, grad_input = summed
    forward_rows = (local_rows[0].astype(jnp.float32) + out_sum).astype(jnp.bfloat16)
    forward_rows = jnp.where(is_encoder, local_carry, forward_rows)
    passed = from_behind(forward_rows[None], seg, 1)
    back = local_carry.astype(jnp.float32) + grad_input
    back_rows = jnp.where(is_encoder, local_carry, back.astype(jnp.bfloat16))
    returned = from_behind(back_rows[None], seg, -1)
    return (passed, returned, kv_grad)


def split_mesh(mesh):
    devices = mesh.devices
    segments = devices.shape[0]
    encoders = segments // 4
    groups = segments // encoders
    try:
        xs = [d.coords[0] for d in devices[0]]
        ys = [d.coords[1] for d in devices[0]]
        wide = len(set(xs))
        tall = devices.shape[1] // wide
        grid_x = np.array(xs).reshape(tall, wide)
        grid_y = np.array(ys).reshape(tall, wide)
        ok = (
            wide * tall == devices.shape[1]
            and wide > 1
            and tall > 1
            and (grid_x == grid_x[:1]).all()
            and (grid_y == grid_y[:, :1]).all()
        )
    except (AttributeError, TypeError, IndexError, ValueError):
        ok = False
    if ok:
        view = devices.reshape(groups, encoders, tall, wide)
        return Mesh(view, ("sg", "sr", "my", "mx")), ("my", "mx"), ("mx", "my")
    view = devices.reshape(groups, encoders, devices.shape[1])
    return Mesh(view, ("sg", "sr", "mp")), "mp", ("mp",)


def solution(mesh):
    inner, mp, stages = split_mesh(mesh)
    seg = ("sg", "sr")
    placed = (
        P(seg, None, None, mp),
        P(seg, None, mp),
        P(seg, None, None, mp),
        P(seg, None, None, None),
    )
    return jax.shard_map(
        functools.partial(per_device, mp, stages),
        mesh=inner,
        in_specs=placed,
        out_specs=(P(seg, None, mp), P(seg, None, mp), P(None, None, mp)),
        check_vma=False,
    )
```

```python
import functools
import math

import numpy as np

import jax
import jax.numpy as jnp
from jax import lax
from jax.sharding import Mesh, PartitionSpec as P

GROUP = 64
NBLEN = 128
NEIGH = 2


def from_behind(x, axis, by):
    devices = lax.axis_size(axis)
    return lax.ppermute(x, axis, [(i, (i + by) % devices) for i in range(devices)])


def attend(queries, key_rows, score_scale):
    scores = (
        jnp.einsum("cqd,ckd->cqk", queries, key_rows, preferred_element_type=jnp.float32)
        * score_scale
    )
    soft = jax.nn.softmax(scores, axis=-1)
    return (soft, soft.astype(jnp.bfloat16))


def attend_back(queries, key_rows, value_rows, soft, rounded, upstream, score_scale):
    d_soft = jnp.einsum("cqd,ckd->cqk", upstream, value_rows, preferred_element_type=jnp.float32)
    grad_values = jnp.einsum("cqk,cqd->ckd", rounded, upstream, preferred_element_type=jnp.float32)
    d_scores = soft * (d_soft - jnp.sum(d_soft * soft, axis=-1, keepdims=True))
    grad_queries = (
        jnp.einsum("cqk,ckd->cqd", d_scores, key_rows.astype(jnp.float32)) * score_scale
    ).astype(jnp.bfloat16)
    grad_keys = jnp.einsum("cqk,cqd->ckd", d_scores, queries.astype(jnp.float32)) * score_scale
    return (grad_queries, grad_keys, grad_values)


def head_sum(terms, axis, tie):
    count, width, tokens = terms.shape
    rounded = terms.astype(jnp.bfloat16)
    if isinstance(axis, tuple):
        tall, wide = lax.axis_size(axis[0]), lax.axis_size(axis[1])
        parts = rounded.reshape(count, tall, wide, width // (tall * wide), tokens).transpose(1, 2, 0, 3, 4)
        partial = lax.psum_scatter(parts, axis[0], scatter_dimension=0, tiled=True)[0]
        partial, tie = lax.optimization_barrier((partial, tie))
        moved = lax.all_to_all(partial, axis[1], 0, 0, tiled=True)
        summed = jnp.sum(moved.astype(jnp.float32), axis=0)
    else:
        devices = lax.axis_size(axis)
        parts = rounded.reshape(count, devices, width // devices, tokens).transpose(1, 0, 2, 3)
        moved = lax.all_to_all(parts, axis, 0, 0, tiled=True)
        summed = jnp.sum(moved.astype(jnp.float32), axis=0)
    return summed.transpose(0, 2, 1), tie


def segment_sum(contrib, axis):
    devices = lax.axis_size(axis)
    parts = contrib.reshape(devices, contrib.shape[0] // devices, contrib.shape[1])
    moved = lax.all_to_all(parts, axis, 0, 0, tiled=True)
    summed = jnp.sum(moved.astype(jnp.float32), axis=0).astype(jnp.bfloat16)
    spread = jnp.broadcast_to(summed[None], (devices,) + summed.shape)
    return lax.all_to_all(spread, axis, 0, 0, tiled=True).reshape(contrib.shape)


def per_device(mp, stages, rows, carry, weights, neighbours):
    seg = ("sg", "sr")
    segments = lax.axis_size(seg)
    encoders = lax.axis_size("sr")
    first_encoder = segments - encoders
    last_group = lax.axis_size("sg") - 1
    group = lax.axis_index("sg")
    is_encoder = group == last_group
    local_rows = rows[0]
    local_carry = carry[0]
    gathered = jnp.concatenate([local_rows, local_carry[None]], axis=0)
    for stage in stages:
        gathered = lax.all_gather(gathered, stage, axis=2, tiled=True)
    full_rows, full_carry = gathered[:2], gathered[2]
    tokens = local_rows.shape[1]
    width = full_rows.shape[2]
    head = weights.shape[3]
    w_query = weights[0, 0]
    w_out = weights[0, 1]

    def encode():
        flat = full_rows.reshape(2 * tokens, width)
        keyval = jnp.concatenate(
            [
                jnp.dot(flat, w_query, preferred_element_type=jnp.float32),
                jnp.dot(flat, w_out, preferred_element_type=jnp.float32),
            ],
            axis=-1,
        ).astype(jnp.bfloat16)
        return (keyval, jnp.zeros((2 * tokens, head), jnp.bfloat16))

    def decode():
        queries = jnp.dot(
            full_rows.reshape(2 * tokens, width), w_query, preferred_element_type=jnp.float32
        ).astype(jnp.bfloat16)
        return (jnp.zeros((2 * tokens, 2 * head), jnp.bfloat16), queries)

    encoded, queries = lax.cond(is_encoder, encode, decode)
    per_encoder = 2 * tokens // NBLEN
    pool_blocks = encoders * per_encoder
    piece = encoded
    for target in range(last_group):
        arrived = lax.ppermute(encoded, "sg", [(last_group, target)])
        piece = jnp.where(group == target, arrived, piece)
    pool = lax.all_gather(piece, "sr", axis=0, tiled=True).reshape(pool_blocks, NBLEN, 2 * head)
    groups = tokens // GROUP
    local_nbr = neighbours[0]
    score_scale = 1.0 / math.sqrt(head)
    query_blocks = queries.reshape(2, groups, GROUP, head)

    def fetch(batch):
        picked = pool[local_nbr[batch]].reshape(groups, NEIGH * NBLEN, 2 * head)
        return (picked[..., :head], picked[..., head:])

    keys_fwd, values_fwd = fetch(0)
    soft_fwd, rounded_fwd = attend(query_blocks[0], keys_fwd, score_scale)
    mixed = jnp.einsum(
        "cqk,ckd->cqd", rounded_fwd, values_fwd, preferred_element_type=jnp.float32
    ).astype(jnp.bfloat16)
    mixed_flat = mixed.reshape(tokens, head)
    upstream = (
        jnp.dot(full_carry, w_out, preferred_element_type=jnp.float32)
        .astype(jnp.bfloat16)
        .reshape(groups, GROUP, head)
    )
    keys_back, values_back = fetch(1)
    soft_back, rounded_back = attend(query_blocks[1], keys_back, score_scale)
    grad_queries, grad_keys, grad_values = attend_back(
        query_blocks[1], keys_back, values_back, soft_back, rounded_back, upstream, score_scale
    )
    grad_flat = grad_queries.reshape(tokens, head)
    terms = jnp.stack(
        [
            lax.dot_general(w_out, mixed_flat, (((1,), (1,)), ((), ())), preferred_element_type=jnp.float32),
            lax.dot_general(w_query, grad_flat, (((1,), (1,)), ((), ())), preferred_element_type=jnp.float32),
        ]
    )
    onehot = (
        local_nbr[1][..., None] == jnp.arange(pool_blocks, dtype=jnp.int32)[None, None, :]
    ).astype(jnp.float32)
    grad_keyval = jnp.concatenate([grad_keys, grad_values], axis=-1).reshape(
        groups, NEIGH, NBLEN, 2 * head
    )
    contrib = jnp.einsum("cbp,cbrf->prf", onehot, grad_keyval)
    contrib = jnp.where(is_encoder, jnp.zeros_like(contrib), contrib)
    pooled = segment_sum(contrib.astype(jnp.bfloat16).reshape(pool_blocks * NBLEN, 2 * head), seg)
    kv_grad = pooled.reshape(pool_blocks * NBLEN, 2, head)
    summed, kv_grad = head_sum(terms, mp, kv_grad)
    out_sum, grad_input = summed
    forward_rows = (local_rows[0].astype(jnp.float32) + out_sum).astype(jnp.bfloat16)
    forward_rows = jnp.where(is_encoder, local_carry, forward_rows)
    passed = from_behind(forward_rows[None], seg, 1)
    back = local_carry.astype(jnp.float32) + grad_input
    back_rows = jnp.where(is_encoder, local_carry, back.astype(jnp.bfloat16))
    returned = from_behind(back_rows[None], seg, -1)
    return (passed, returned, kv_grad)


def split_mesh(mesh):
    devices = mesh.devices
    segments = devices.shape[0]
    encoders = segments // 4
    groups = segments // encoders
    try:
        xs = [d.coords[0] for d in devices[0]]
        ys = [d.coords[1] for d in devices[0]]
        wide = len(set(xs))
        tall = devices.shape[1] // wide
        grid_x = np.array(xs).reshape(tall, wide)
        grid_y = np.array(ys).reshape(tall, wide)
        ok = (
            wide * tall == devices.shape[1]
            and wide > 1
            and tall > 1
            and (grid_x == grid_x[:1]).all()
            and (grid_y == grid_y[:, :1]).all()
        )
    except (AttributeError, TypeError, IndexError, ValueError):
        ok = False
    if ok:
        view = devices.reshape(groups, encoders, tall, wide)
        return Mesh(view, ("sg", "sr", "my", "mx")), ("my", "mx"), ("mx", "my")
    view = devices.reshape(groups, encoders, devices.shape[1])
    return Mesh(view, ("sg", "sr", "mp")), "mp", ("mp",)


def solution(mesh):
    inner, mp, stages = split_mesh(mesh)
    seg = ("sg", "sr")
    placed = (
        P(seg, None, None, mp),
        P(seg, None, mp),
        P(seg, None, None, mp),
        P(seg, None, None, None),
    )
    return jax.shard_map(
        functools.partial(per_device, mp, stages),
        mesh=inner,
        in_specs=placed,
        out_specs=(P(seg, None, mp), P(seg, None, mp), P(None, None, mp)),
        check_vma=False,
    )
```

```python
import functools
import math

import numpy as np

import jax
import jax.numpy as jnp
from jax import lax
from jax.sharding import Mesh, PartitionSpec as P

GROUP = 64
NBLEN = 128
NEIGH = 2


def from_behind(x, axis, by):
    devices = lax.axis_size(axis)
    return lax.ppermute(x, axis, [(i, (i + by) % devices) for i in range(devices)])


def attend(queries, key_rows, score_scale):
    scores = (
        jnp.einsum("cqd,ckd->cqk", queries, key_rows, preferred_element_type=jnp.float32)
        * score_scale
    )
    soft = jax.nn.softmax(scores, axis=-1)
    return (soft, soft.astype(jnp.bfloat16))


def attend_back(queries, key_rows, value_rows, soft, rounded, upstream, score_scale):
    d_soft = jnp.einsum("cqd,ckd->cqk", upstream, value_rows, preferred_element_type=jnp.float32)
    grad_values = jnp.einsum("cqk,cqd->ckd", rounded, upstream, preferred_element_type=jnp.float32)
    d_scores = soft * (d_soft - jnp.sum(d_soft * soft, axis=-1, keepdims=True))
    grad_queries = (
        jnp.einsum("cqk,ckd->cqd", d_scores, key_rows.astype(jnp.float32)) * score_scale
    ).astype(jnp.bfloat16)
    grad_keys = jnp.einsum("cqk,cqd->ckd", d_scores, queries.astype(jnp.float32)) * score_scale
    return (grad_queries, grad_keys, grad_values)


def head_sum(terms, axis, tie):
    count, width, tokens = terms.shape
    rounded = terms.astype(jnp.bfloat16)
    if isinstance(axis, tuple):
        tall, wide = lax.axis_size(axis[0]), lax.axis_size(axis[1])
        parts = rounded.reshape(count, tall, wide, width // (tall * wide), tokens).transpose(1, 2, 0, 3, 4)
        partial = lax.psum_scatter(parts, axis[0], scatter_dimension=0, tiled=True)[0]
        partial, tie = lax.optimization_barrier((partial, tie))
        moved = lax.all_to_all(partial, axis[1], 0, 0, tiled=True)
        summed = jnp.sum(moved.astype(jnp.float32), axis=0)
    else:
        devices = lax.axis_size(axis)
        parts = rounded.reshape(count, devices, width // devices, tokens).transpose(1, 0, 2, 3)
        moved = lax.all_to_all(parts, axis, 0, 0, tiled=True)
        summed = jnp.sum(moved.astype(jnp.float32), axis=0)
    return summed.transpose(0, 2, 1), tie


def segment_sum(contrib, axis):
    devices = lax.axis_size(axis)
    parts = contrib.reshape(devices, contrib.shape[0] // devices, contrib.shape[1])
    moved = lax.all_to_all(parts, axis, 0, 0, tiled=True)
    summed = jnp.sum(moved.astype(jnp.float32), axis=0).astype(jnp.bfloat16)
    spread = jnp.broadcast_to(summed[None], (devices,) + summed.shape)
    return lax.all_to_all(spread, axis, 0, 0, tiled=True).reshape(contrib.shape)


def per_device(mp, stages, rows, carry, weights, neighbours):
    seg = ("sg", "sr")
    segments = lax.axis_size(seg)
    encoders = lax.axis_size("sr")
    first_encoder = segments - encoders
    last_group = lax.axis_size("sg") - 1
    group = lax.axis_index("sg")
    is_encoder = group == last_group
    local_rows = rows[0]
    local_carry = carry[0]
    full_rows, full_carry = local_rows, local_carry
    for stage in stages:
        full_rows = lax.all_gather(full_rows, stage, axis=2, tiled=True)
    for stage in stages:
        full_carry = lax.all_gather(full_carry, stage, axis=1, tiled=True)
    tokens = local_rows.shape[1]
    width = full_rows.shape[2]
    head = weights.shape[3]
    w_query = weights[0, 0]
    w_out = weights[0, 1]

    def encode():
        flat = full_rows.reshape(2 * tokens, width)
        keyval = jnp.concatenate(
            [
                jnp.dot(flat, w_query, preferred_element_type=jnp.float32),
                jnp.dot(flat, w_out, preferred_element_type=jnp.float32),
            ],
            axis=-1,
        ).astype(jnp.bfloat16)
        return (keyval, jnp.zeros((2 * tokens, head), jnp.bfloat16))

    def decode():
        queries = jnp.dot(
            full_rows.reshape(2 * tokens, width), w_query, preferred_element_type=jnp.float32
        ).astype(jnp.bfloat16)
        return (jnp.zeros((2 * tokens, 2 * head), jnp.bfloat16), queries)

    encoded, queries = lax.cond(is_encoder, encode, decode)
    per_encoder = 2 * tokens // NBLEN
    pool_blocks = encoders * per_encoder
    piece = encoded
    for target in range(last_group):
        arrived = lax.ppermute(encoded, "sg", [(last_group, target)])
        piece = jnp.where(group == target, arrived, piece)
    pool = lax.all_gather(piece, "sr", axis=0, tiled=True).reshape(pool_blocks, NBLEN, 2 * head)
    groups = tokens // GROUP
    local_nbr = neighbours[0]
    score_scale = 1.0 / math.sqrt(head)
    query_blocks = queries.reshape(2, groups, GROUP, head)

    def fetch(batch):
        picked = pool[local_nbr[batch]].reshape(groups, NEIGH * NBLEN, 2 * head)
        return (picked[..., :head], picked[..., head:])

    keys_fwd, values_fwd = fetch(0)
    soft_fwd, rounded_fwd = attend(query_blocks[0], keys_fwd, score_scale)
    mixed = jnp.einsum(
        "cqk,ckd->cqd", rounded_fwd, values_fwd, preferred_element_type=jnp.float32
    ).astype(jnp.bfloat16)
    mixed_flat = mixed.reshape(tokens, head)
    upstream = (
        jnp.dot(full_carry, w_out, preferred_element_type=jnp.float32)
        .astype(jnp.bfloat16)
        .reshape(groups, GROUP, head)
    )
    keys_back, values_back = fetch(1)
    soft_back, rounded_back = attend(query_blocks[1], keys_back, score_scale)
    grad_queries, grad_keys, grad_values = attend_back(
        query_blocks[1], keys_back, values_back, soft_back, rounded_back, upstream, score_scale
    )
    grad_flat = grad_queries.reshape(tokens, head)
    terms = jnp.stack(
        [
            lax.dot_general(w_out, mixed_flat, (((1,), (1,)), ((), ())), preferred_element_type=jnp.float32),
            lax.dot_general(w_query, grad_flat, (((1,), (1,)), ((), ())), preferred_element_type=jnp.float32),
        ]
    )
    onehot = (
        local_nbr[1][..., None] == jnp.arange(pool_blocks, dtype=jnp.int32)[None, None, :]
    ).astype(jnp.float32)
    grad_keyval = jnp.concatenate([grad_keys, grad_values], axis=-1).reshape(
        groups, NEIGH, NBLEN, 2 * head
    )
    contrib = jnp.einsum("cbp,cbrf->prf", onehot, grad_keyval)
    contrib = jnp.where(is_encoder, jnp.zeros_like(contrib), contrib)
    pooled = segment_sum(contrib.astype(jnp.bfloat16).reshape(pool_blocks * NBLEN, 2 * head), seg)
    kv_grad = pooled.reshape(pool_blocks * NBLEN, 2, head)
    summed, kv_grad = head_sum(terms, mp, kv_grad)
    out_sum, grad_input = summed
    forward_rows = (local_rows[0].astype(jnp.float32) + out_sum).astype(jnp.bfloat16)
    forward_rows = jnp.where(is_encoder, local_carry, forward_rows)
    passed = from_behind(forward_rows[None], seg, 1)
    back = local_carry.astype(jnp.float32) + grad_input
    back_rows = jnp.where(is_encoder, local_carry, back.astype(jnp.bfloat16))
    returned = from_behind(back_rows[None], seg, -1)
    return (passed, returned, kv_grad)


def split_mesh(mesh):
    devices = mesh.devices
    segments = devices.shape[0]
    encoders = segments // 4
    groups = segments // encoders
    try:
        xs = [d.coords[0] for d in devices[0]]
        ys = [d.coords[1] for d in devices[0]]
        wide = len(set(xs))
        tall = devices.shape[1] // wide
        grid_x = np.array(xs).reshape(tall, wide)
        grid_y = np.array(ys).reshape(tall, wide)
        ok = (
            wide * tall == devices.shape[1]
            and wide > 1
            and tall > 1
            and (grid_x == grid_x[:1]).all()
            and (grid_y == grid_y[:, :1]).all()
        )
    except (AttributeError, TypeError, IndexError, ValueError):
        ok = False
    if ok:
        view = devices.reshape(groups, encoders, tall, wide)
        return Mesh(view, ("sg", "sr", "my", "mx")), ("my", "mx"), ("mx", "my")
    view = devices.reshape(groups, encoders, devices.shape[1])
    return Mesh(view, ("sg", "sr", "mp")), "mp", ("mp",)


def solution(mesh):
    inner, mp, stages = split_mesh(mesh)
    seg = ("sg", "sr")
    placed = (
        P(seg, None, None, mp),
        P(seg, None, mp),
        P(seg, None, None, mp),
        P(seg, None, None, None),
    )
    return jax.shard_map(
        functools.partial(per_device, mp, stages),
        mesh=inner,
        in_specs=placed,
        out_specs=(P(seg, None, mp), P(seg, None, mp), P(None, None, mp)),
        check_vma=False,
    )
```

```python
import functools
import math

import numpy as np

import jax
import jax.numpy as jnp
from jax import lax
from jax.sharding import Mesh, PartitionSpec as P

GROUP = 64
NBLEN = 128
NEIGH = 2


def from_behind(x, axis, by):
    devices = lax.axis_size(axis)
    return lax.ppermute(x, axis, [(i, (i + by) % devices) for i in range(devices)])


def attend(queries, key_rows, score_scale):
    scores = (
        jnp.einsum("cqd,ckd->cqk", queries, key_rows, preferred_element_type=jnp.float32)
        * score_scale
    )
    soft = jax.nn.softmax(scores, axis=-1)
    return (soft, soft.astype(jnp.bfloat16))


def attend_back(queries, key_rows, value_rows, soft, rounded, upstream, score_scale):
    d_soft = jnp.einsum("cqd,ckd->cqk", upstream, value_rows, preferred_element_type=jnp.float32)
    grad_values = jnp.einsum("cqk,cqd->ckd", rounded, upstream, preferred_element_type=jnp.float32)
    d_scores = soft * (d_soft - jnp.sum(d_soft * soft, axis=-1, keepdims=True))
    grad_queries = (
        jnp.einsum("cqk,ckd->cqd", d_scores, key_rows.astype(jnp.float32)) * score_scale
    ).astype(jnp.bfloat16)
    grad_keys = jnp.einsum("cqk,cqd->ckd", d_scores, queries.astype(jnp.float32)) * score_scale
    return (grad_queries, grad_keys, grad_values)


def head_sum(terms, axis, tie):
    count, width, tokens = terms.shape
    rounded = terms.astype(jnp.bfloat16)
    if isinstance(axis, tuple):
        tall, wide = lax.axis_size(axis[0]), lax.axis_size(axis[1])
        parts = rounded.reshape(count, tall, wide, width // (tall * wide), tokens).transpose(1, 2, 0, 3, 4)
        partial = lax.psum_scatter(parts, axis[0], scatter_dimension=0, tiled=True)[0]
        partial, tie = lax.optimization_barrier((partial, tie))
        moved = lax.all_to_all(partial, axis[1], 0, 0, tiled=True)
        summed = jnp.sum(moved.astype(jnp.float32), axis=0)
    else:
        devices = lax.axis_size(axis)
        parts = rounded.reshape(count, devices, width // devices, tokens).transpose(1, 0, 2, 3)
        moved = lax.all_to_all(parts, axis, 0, 0, tiled=True)
        summed = jnp.sum(moved.astype(jnp.float32), axis=0)
    return summed.transpose(0, 2, 1), tie


def segment_sum(contrib, axis):
    devices = lax.axis_size(axis)
    parts = contrib.reshape(devices, contrib.shape[0] // devices, contrib.shape[1])
    moved = lax.all_to_all(parts, axis, 0, 0, tiled=True)
    summed = jnp.sum(moved.astype(jnp.float32), axis=0).astype(jnp.bfloat16)
    spread = jnp.broadcast_to(summed[None], (devices,) + summed.shape)
    return lax.all_to_all(spread, axis, 0, 0, tiled=True).reshape(contrib.shape)


def per_device(mp, stages, rows, carry, weights, neighbours):
    seg = ("sg", "sr")
    segments = lax.axis_size(seg)
    encoders = lax.axis_size("sr")
    first_encoder = segments - encoders
    last_group = lax.axis_size("sg") - 1
    group = lax.axis_index("sg")
    is_encoder = group == last_group
    local_rows = rows[0]
    local_carry = carry[0]
    gathered = jnp.concatenate([local_rows, local_carry[None]], axis=0)
    for stage in stages:
        gathered = lax.all_gather(gathered, stage, axis=2, tiled=True)
    full_rows, full_carry = gathered[:2], gathered[2]
    tokens = local_rows.shape[1]
    width = full_rows.shape[2]
    head = weights.shape[3]
    w_query = weights[0, 0]
    w_out = weights[0, 1]

    def encode():
        flat = full_rows.reshape(2 * tokens, width)
        keyval = jnp.concatenate(
            [
                jnp.dot(flat, w_query, preferred_element_type=jnp.float32),
                jnp.dot(flat, w_out, preferred_element_type=jnp.float32),
            ],
            axis=-1,
        ).astype(jnp.bfloat16)
        return (keyval, jnp.zeros((2 * tokens, head), jnp.bfloat16))

    def decode():
        queries = jnp.dot(
            full_rows.reshape(2 * tokens, width), w_query, preferred_element_type=jnp.float32
        ).astype(jnp.bfloat16)
        return (jnp.zeros((2 * tokens, 2 * head), jnp.bfloat16), queries)

    encoded, queries = lax.cond(is_encoder, encode, decode)
    per_encoder = 2 * tokens // NBLEN
    pool_blocks = encoders * per_encoder
    piece = encoded
    for target in range(last_group):
        arrived = lax.ppermute(encoded, "sg", [(last_group, target)])
        piece = jnp.where(group == target, arrived, piece)
    places = lax.axis_size("sr")
    spot = lax.axis_index("sr")
    held = [piece] + [
        lax.ppermute(piece, "sr", [(i, (i + shift) % places) for i in range(places)])
        for shift in range(1, places)
    ]
    ordered = jnp.roll(jnp.stack(held[::-1]), spot + 1, axis=0)
    pool = ordered.reshape(pool_blocks, NBLEN, 2 * head)
    groups = tokens // GROUP
    local_nbr = neighbours[0]
    score_scale = 1.0 / math.sqrt(head)
    query_blocks = queries.reshape(2, groups, GROUP, head)

    def fetch(batch):
        picked = pool[local_nbr[batch]].reshape(groups, NEIGH * NBLEN, 2 * head)
        return (picked[..., :head], picked[..., head:])

    keys_fwd, values_fwd = fetch(0)
    soft_fwd, rounded_fwd = attend(query_blocks[0], keys_fwd, score_scale)
    mixed = jnp.einsum(
        "cqk,ckd->cqd", rounded_fwd, values_fwd, preferred_element_type=jnp.float32
    ).astype(jnp.bfloat16)
    mixed_flat = mixed.reshape(tokens, head)
    upstream = (
        jnp.dot(full_carry, w_out, preferred_element_type=jnp.float32)
        .astype(jnp.bfloat16)
        .reshape(groups, GROUP, head)
    )
    keys_back, values_back = fetch(1)
    soft_back, rounded_back = attend(query_blocks[1], keys_back, score_scale)
    grad_queries, grad_keys, grad_values = attend_back(
        query_blocks[1], keys_back, values_back, soft_back, rounded_back, upstream, score_scale
    )
    grad_flat = grad_queries.reshape(tokens, head)
    terms = jnp.stack(
        [
            lax.dot_general(w_out, mixed_flat, (((1,), (1,)), ((), ())), preferred_element_type=jnp.float32),
            lax.dot_general(w_query, grad_flat, (((1,), (1,)), ((), ())), preferred_element_type=jnp.float32),
        ]
    )
    onehot = (
        local_nbr[1][..., None] == jnp.arange(pool_blocks, dtype=jnp.int32)[None, None, :]
    ).astype(jnp.float32)
    grad_keyval = jnp.concatenate([grad_keys, grad_values], axis=-1).reshape(
        groups, NEIGH, NBLEN, 2 * head
    )
    contrib = jnp.einsum("cbp,cbrf->prf", onehot, grad_keyval)
    contrib = jnp.where(is_encoder, jnp.zeros_like(contrib), contrib)
    pooled = segment_sum(contrib.astype(jnp.bfloat16).reshape(pool_blocks * NBLEN, 2 * head), seg)
    kv_grad = pooled.reshape(pool_blocks * NBLEN, 2, head)
    summed, kv_grad = head_sum(terms, mp, kv_grad)
    out_sum, grad_input = summed
    forward_rows = (local_rows[0].astype(jnp.float32) + out_sum).astype(jnp.bfloat16)
    forward_rows = jnp.where(is_encoder, local_carry, forward_rows)
    passed = from_behind(forward_rows[None], seg, 1)
    back = local_carry.astype(jnp.float32) + grad_input
    back_rows = jnp.where(is_encoder, local_carry, back.astype(jnp.bfloat16))
    returned = from_behind(back_rows[None], seg, -1)
    return (passed, returned, kv_grad)


def split_mesh(mesh):
    devices = mesh.devices
    segments = devices.shape[0]
    encoders = segments // 4
    groups = segments // encoders
    try:
        xs = [d.coords[0] for d in devices[0]]
        ys = [d.coords[1] for d in devices[0]]
        wide = len(set(xs))
        tall = devices.shape[1] // wide
        grid_x = np.array(xs).reshape(tall, wide)
        grid_y = np.array(ys).reshape(tall, wide)
        ok = (
            wide * tall == devices.shape[1]
            and wide > 1
            and tall > 1
            and (grid_x == grid_x[:1]).all()
            and (grid_y == grid_y[:, :1]).all()
        )
    except (AttributeError, TypeError, IndexError, ValueError):
        ok = False
    if ok:
        view = devices.reshape(groups, encoders, tall, wide)
        return Mesh(view, ("sg", "sr", "my", "mx")), ("my", "mx"), ("mx", "my")
    view = devices.reshape(groups, encoders, devices.shape[1])
    return Mesh(view, ("sg", "sr", "mp")), "mp", ("mp",)


def solution(mesh):
    inner, mp, stages = split_mesh(mesh)
    seg = ("sg", "sr")
    placed = (
        P(seg, None, None, mp),
        P(seg, None, mp),
        P(seg, None, None, mp),
        P(seg, None, None, None),
    )
    return jax.shard_map(
        functools.partial(per_device, mp, stages),
        mesh=inner,
        in_specs=placed,
        out_specs=(P(seg, None, mp), P(seg, None, mp), P(None, None, mp)),
        check_vma=False,
    )
```

```python
import functools
import math

import numpy as np

import jax
import jax.numpy as jnp
from jax import lax
from jax.sharding import Mesh, PartitionSpec as P

GROUP = 64
NBLEN = 128
NEIGH = 2


def from_behind(x, axis, by):
    devices = lax.axis_size(axis)
    return lax.ppermute(x, axis, [(i, (i + by) % devices) for i in range(devices)])


def attend(queries, key_rows, score_scale):
    scores = (
        jnp.einsum("cqd,ckd->cqk", queries, key_rows, preferred_element_type=jnp.float32)
        * score_scale
    )
    soft = jax.nn.softmax(scores, axis=-1)
    return (soft, soft.astype(jnp.bfloat16))


def attend_back(queries, key_rows, value_rows, soft, rounded, upstream, score_scale):
    d_soft = jnp.einsum("cqd,ckd->cqk", upstream, value_rows, preferred_element_type=jnp.float32)
    grad_values = jnp.einsum("cqk,cqd->ckd", rounded, upstream, preferred_element_type=jnp.float32)
    d_scores = soft * (d_soft - jnp.sum(d_soft * soft, axis=-1, keepdims=True))
    grad_queries = (
        jnp.einsum("cqk,ckd->cqd", d_scores, key_rows.astype(jnp.float32)) * score_scale
    ).astype(jnp.bfloat16)
    grad_keys = jnp.einsum("cqk,cqd->ckd", d_scores, queries.astype(jnp.float32)) * score_scale
    return (grad_queries, grad_keys, grad_values)


def head_sum(terms, axis, tie):
    count, width, tokens = terms.shape
    rounded = terms.astype(jnp.bfloat16)
    if isinstance(axis, tuple):
        tall, wide = lax.axis_size(axis[0]), lax.axis_size(axis[1])
        parts = tuple(r.reshape(tall, wide, width // (tall * wide), tokens) for r in rounded)
        scattered = lax.psum_scatter(parts, axis[0], scatter_dimension=0, tiled=True)
        partial = jnp.stack([p[0] for p in scattered], axis=1)
        partial, tie = lax.optimization_barrier((partial, tie))
        moved = lax.all_to_all(partial, axis[1], 0, 0, tiled=True)
        summed = jnp.sum(moved.astype(jnp.float32), axis=0)
    else:
        devices = lax.axis_size(axis)
        parts = rounded.reshape(count, devices, width // devices, tokens).transpose(1, 0, 2, 3)
        moved = lax.all_to_all(parts, axis, 0, 0, tiled=True)
        summed = jnp.sum(moved.astype(jnp.float32), axis=0)
    return summed.transpose(0, 2, 1), tie


def segment_sum(contrib, axis):
    devices = lax.axis_size(axis)
    parts = contrib.reshape(devices, contrib.shape[0] // devices, contrib.shape[1])
    moved = lax.all_to_all(parts, axis, 0, 0, tiled=True)
    summed = jnp.sum(moved.astype(jnp.float32), axis=0).astype(jnp.bfloat16)
    spread = jnp.broadcast_to(summed[None], (devices,) + summed.shape)
    return lax.all_to_all(spread, axis, 0, 0, tiled=True).reshape(contrib.shape)


def per_device(mp, stages, rows, carry, weights, neighbours):
    seg = ("sg", "sr")
    segments = lax.axis_size(seg)
    encoders = lax.axis_size("sr")
    first_encoder = segments - encoders
    last_group = lax.axis_size("sg") - 1
    group = lax.axis_index("sg")
    is_encoder = group == last_group
    local_rows = rows[0]
    local_carry = carry[0]
    gathered = jnp.concatenate([local_rows, local_carry[None]], axis=0)
    for stage in stages:
        gathered = lax.all_gather(gathered, stage, axis=2, tiled=True)
    full_rows, full_carry = gathered[:2], gathered[2]
    tokens = local_rows.shape[1]
    width = full_rows.shape[2]
    head = weights.shape[3]
    w_query = weights[0, 0]
    w_out = weights[0, 1]

    def encode():
        flat = full_rows.reshape(2 * tokens, width)
        keyval = jnp.concatenate(
            [
                jnp.dot(flat, w_query, preferred_element_type=jnp.float32),
                jnp.dot(flat, w_out, preferred_element_type=jnp.float32),
            ],
            axis=-1,
        ).astype(jnp.bfloat16)
        return (keyval, jnp.zeros((2 * tokens, head), jnp.bfloat16))

    def decode():
        queries = jnp.dot(
            full_rows.reshape(2 * tokens, width), w_query, preferred_element_type=jnp.float32
        ).astype(jnp.bfloat16)
        return (jnp.zeros((2 * tokens, 2 * head), jnp.bfloat16), queries)

    encoded, queries = lax.cond(is_encoder, encode, decode)
    per_encoder = 2 * tokens // NBLEN
    pool_blocks = encoders * per_encoder
    piece = encoded
    for target in range(last_group):
        arrived = lax.ppermute(encoded, "sg", [(last_group, target)])
        piece = jnp.where(group == target, arrived, piece)
    pool = lax.all_gather(piece, "sr", axis=0, tiled=True).reshape(pool_blocks, NBLEN, 2 * head)
    groups = tokens // GROUP
    local_nbr = neighbours[0]
    score_scale = 1.0 / math.sqrt(head)
    query_blocks = queries.reshape(2, groups, GROUP, head)

    def fetch(batch):
        picked = pool[local_nbr[batch]].reshape(groups, NEIGH * NBLEN, 2 * head)
        return (picked[..., :head], picked[..., head:])

    keys_fwd, values_fwd = fetch(0)
    soft_fwd, rounded_fwd = attend(query_blocks[0], keys_fwd, score_scale)
    mixed = jnp.einsum(
        "cqk,ckd->cqd", rounded_fwd, values_fwd, preferred_element_type=jnp.float32
    ).astype(jnp.bfloat16)
    mixed_flat = mixed.reshape(tokens, head)
    upstream = (
        jnp.dot(full_carry, w_out, preferred_element_type=jnp.float32)
        .astype(jnp.bfloat16)
        .reshape(groups, GROUP, head)
    )
    keys_back, values_back = fetch(1)
    soft_back, rounded_back = attend(query_blocks[1], keys_back, score_scale)
    grad_queries, grad_keys, grad_values = attend_back(
        query_blocks[1], keys_back, values_back, soft_back, rounded_back, upstream, score_scale
    )
    grad_flat = grad_queries.reshape(tokens, head)
    terms = jnp.stack(
        [
            lax.dot_general(w_out, mixed_flat, (((1,), (1,)), ((), ())), preferred_element_type=jnp.float32),
            lax.dot_general(w_query, grad_flat, (((1,), (1,)), ((), ())), preferred_element_type=jnp.float32),
        ]
    )
    onehot = (
        local_nbr[1][..., None] == jnp.arange(pool_blocks, dtype=jnp.int32)[None, None, :]
    ).astype(jnp.float32)
    grad_keyval = jnp.concatenate([grad_keys, grad_values], axis=-1).reshape(
        groups, NEIGH, NBLEN, 2 * head
    )
    contrib = jnp.einsum("cbp,cbrf->prf", onehot, grad_keyval)
    contrib = jnp.where(is_encoder, jnp.zeros_like(contrib), contrib)
    pooled = segment_sum(contrib.astype(jnp.bfloat16).reshape(pool_blocks * NBLEN, 2 * head), seg)
    kv_grad = pooled.reshape(pool_blocks * NBLEN, 2, head)
    summed, kv_grad = head_sum(terms, mp, kv_grad)
    out_sum, grad_input = summed
    forward_rows = (local_rows[0].astype(jnp.float32) + out_sum).astype(jnp.bfloat16)
    forward_rows = jnp.where(is_encoder, local_carry, forward_rows)
    passed = from_behind(forward_rows[None], seg, 1)
    back = local_carry.astype(jnp.float32) + grad_input
    back_rows = jnp.where(is_encoder, local_carry, back.astype(jnp.bfloat16))
    returned = from_behind(back_rows[None], seg, -1)
    return (passed, returned, kv_grad)


def split_mesh(mesh):
    devices = mesh.devices
    segments = devices.shape[0]
    encoders = segments // 4
    groups = segments // encoders
    try:
        xs = [d.coords[0] for d in devices[0]]
        ys = [d.coords[1] for d in devices[0]]
        wide = len(set(xs))
        tall = devices.shape[1] // wide
        grid_x = np.array(xs).reshape(tall, wide)
        grid_y = np.array(ys).reshape(tall, wide)
        ok = (
            wide * tall == devices.shape[1]
            and wide > 1
            and tall > 1
            and (grid_x == grid_x[:1]).all()
            and (grid_y == grid_y[:, :1]).all()
        )
    except (AttributeError, TypeError, IndexError, ValueError):
        ok = False
    if ok:
        view = devices.reshape(groups, encoders, tall, wide)
        return Mesh(view, ("sg", "sr", "my", "mx")), ("my", "mx"), ("mx", "my")
    view = devices.reshape(groups, encoders, devices.shape[1])
    return Mesh(view, ("sg", "sr", "mp")), "mp", ("mp",)


def solution(mesh):
    inner, mp, stages = split_mesh(mesh)
    seg = ("sg", "sr")
    placed = (
        P(seg, None, None, mp),
        P(seg, None, mp),
        P(seg, None, None, mp),
        P(seg, None, None, None),
    )
    return jax.shard_map(
        functools.partial(per_device, mp, stages),
        mesh=inner,
        in_specs=placed,
        out_specs=(P(seg, None, mp), P(seg, None, mp), P(None, None, mp)),
        check_vma=False,
    )
```

```python
import functools
import math

import numpy as np

import jax
import jax.numpy as jnp
from jax import lax
from jax.sharding import Mesh, PartitionSpec as P

GROUP = 64
NBLEN = 128
NEIGH = 2


def from_behind(x, axis, by):
    devices = lax.axis_size(axis)
    return lax.ppermute(x, axis, [(i, (i + by) % devices) for i in range(devices)])


def attend(queries, key_rows, score_scale):
    scores = (
        jnp.einsum("cqd,ckd->cqk", queries, key_rows, preferred_element_type=jnp.float32)
        * score_scale
    )
    soft = jax.nn.softmax(scores, axis=-1)
    return (soft, soft.astype(jnp.bfloat16))


def attend_back(queries, key_rows, value_rows, soft, rounded, upstream, score_scale):
    d_soft = jnp.einsum("cqd,ckd->cqk", upstream, value_rows, preferred_element_type=jnp.float32)
    grad_values = jnp.einsum("cqk,cqd->ckd", rounded, upstream, preferred_element_type=jnp.float32)
    d_scores = soft * (d_soft - jnp.sum(d_soft * soft, axis=-1, keepdims=True))
    grad_queries = (
        jnp.einsum("cqk,ckd->cqd", d_scores, key_rows.astype(jnp.float32)) * score_scale
    ).astype(jnp.bfloat16)
    grad_keys = jnp.einsum("cqk,cqd->ckd", d_scores, queries.astype(jnp.float32)) * score_scale
    return (grad_queries, grad_keys, grad_values)


def head_sum(terms, axis, tie):
    count, width, tokens = terms.shape
    rounded = terms.astype(jnp.bfloat16)
    if isinstance(axis, tuple):
        tall, wide = lax.axis_size(axis[0]), lax.axis_size(axis[1])
        parts = rounded.reshape(count, tall, wide, width // (tall * wide), tokens).transpose(1, 2, 0, 3, 4)
        partial = lax.psum_scatter(parts, axis[0], scatter_dimension=0, tiled=True)[0]
        partial, tie = lax.optimization_barrier((partial, tie))
        moved = lax.all_to_all(partial, axis[1], 0, 0, tiled=True)
        summed = jnp.sum(moved.astype(jnp.float32), axis=0)
    else:
        devices = lax.axis_size(axis)
        parts = rounded.reshape(count, devices, width // devices, tokens).transpose(1, 0, 2, 3)
        moved = lax.all_to_all(parts, axis, 0, 0, tiled=True)
        summed = jnp.sum(moved.astype(jnp.float32), axis=0)
    return summed.transpose(0, 2, 1), tie


def segment_sum(contrib, axis):
    devices = lax.axis_size(axis)
    parts = contrib.reshape(devices, contrib.shape[0] // devices, contrib.shape[1])
    moved = lax.all_to_all(parts, axis, 0, 0, tiled=True)
    summed = jnp.sum(moved.astype(jnp.float32), axis=0).astype(jnp.bfloat16)
    spread = jnp.broadcast_to(summed[None], (devices,) + summed.shape)
    return lax.all_to_all(spread, axis, 0, 0, tiled=True).reshape(contrib.shape)


def per_device(mp, stages, rows, carry, weights, neighbours):
    seg = ("sg", "sr")
    segments = lax.axis_size(seg)
    encoders = lax.axis_size("sr")
    first_encoder = segments - encoders
    last_group = lax.axis_size("sg") - 1
    group = lax.axis_index("sg")
    is_encoder = group == last_group
    local_rows = rows[0]
    local_carry = carry[0]
    gathered = jnp.concatenate([local_rows, local_carry[None]], axis=0)
    for stage in stages:
        gathered = lax.all_gather(gathered, stage, axis=2, tiled=True)
    full_rows, full_carry = gathered[:2], gathered[2]
    tokens = local_rows.shape[1]
    width = full_rows.shape[2]
    head = weights.shape[3]
    w_query = weights[0, 0]
    w_out = weights[0, 1]

    def encode():
        flat = full_rows.reshape(2 * tokens, width)
        keyval = jnp.concatenate(
            [
                jnp.dot(flat, w_query, preferred_element_type=jnp.float32),
                jnp.dot(flat, w_out, preferred_element_type=jnp.float32),
            ],
            axis=-1,
        ).astype(jnp.bfloat16)
        return (keyval, jnp.zeros((2 * tokens, head), jnp.bfloat16))

    def decode():
        queries = jnp.dot(
            full_rows.reshape(2 * tokens, width), w_query, preferred_element_type=jnp.float32
        ).astype(jnp.bfloat16)
        return (jnp.zeros((2 * tokens, 2 * head), jnp.bfloat16), queries)

    encoded, queries = lax.cond(is_encoder, encode, decode)
    per_encoder = 2 * tokens // NBLEN
    pool_blocks = encoders * per_encoder
    piece = encoded
    for target in range(last_group):
        arrived = lax.ppermute(encoded, "sg", [(last_group, target)])
        piece = jnp.where(group == target, arrived, piece)
    pool = lax.all_gather(piece, "sr", axis=0, tiled=True).reshape(pool_blocks, NBLEN, 2 * head)
    groups = tokens // GROUP
    local_nbr = neighbours[0]
    score_scale = 1.0 / math.sqrt(head)
    query_blocks = queries.reshape(2, groups, GROUP, head)

    def fetch(batch):
        picked = pool[local_nbr[batch]].reshape(groups, NEIGH * NBLEN, 2 * head)
        return (picked[..., :head], picked[..., head:])

    keys_fwd, values_fwd = fetch(0)
    soft_fwd, rounded_fwd = attend(query_blocks[0], keys_fwd, score_scale)
    mixed = jnp.einsum(
        "cqk,ckd->cqd", rounded_fwd, values_fwd, preferred_element_type=jnp.float32
    ).astype(jnp.bfloat16)
    mixed_flat = mixed.reshape(tokens, head)
    upstream = (
        jnp.dot(full_carry, w_out, preferred_element_type=jnp.float32)
        .astype(jnp.bfloat16)
        .reshape(groups, GROUP, head)
    )
    keys_back, values_back = fetch(1)
    soft_back, rounded_back = attend(query_blocks[1], keys_back, score_scale)
    grad_queries, grad_keys, grad_values = attend_back(
        query_blocks[1], keys_back, values_back, soft_back, rounded_back, upstream, score_scale
    )
    grad_flat = grad_queries.reshape(tokens, head)
    terms = jnp.einsum(
        "kfd,ktd->kft",
        weights[0][::-1],
        jnp.stack([mixed_flat, grad_flat]),
        preferred_element_type=jnp.float32,
    )
    onehot = (
        local_nbr[1][..., None] == jnp.arange(pool_blocks, dtype=jnp.int32)[None, None, :]
    ).astype(jnp.float32)
    grad_keyval = jnp.concatenate([grad_keys, grad_values], axis=-1).reshape(
        groups, NEIGH, NBLEN, 2 * head
    )
    contrib = jnp.einsum("cbp,cbrf->prf", onehot, grad_keyval)
    contrib = jnp.where(is_encoder, jnp.zeros_like(contrib), contrib)
    pooled = segment_sum(contrib.astype(jnp.bfloat16).reshape(pool_blocks * NBLEN, 2 * head), seg)
    kv_grad = pooled.reshape(pool_blocks * NBLEN, 2, head)
    summed, kv_grad = head_sum(terms, mp, kv_grad)
    out_sum, grad_input = summed
    forward_rows = (local_rows[0].astype(jnp.float32) + out_sum).astype(jnp.bfloat16)
    forward_rows = jnp.where(is_encoder, local_carry, forward_rows)
    passed = from_behind(forward_rows[None], seg, 1)
    back = local_carry.astype(jnp.float32) + grad_input
    back_rows = jnp.where(is_encoder, local_carry, back.astype(jnp.bfloat16))
    returned = from_behind(back_rows[None], seg, -1)
    return (passed, returned, kv_grad)


def split_mesh(mesh):
    devices = mesh.devices
    segments = devices.shape[0]
    encoders = segments // 4
    groups = segments // encoders
    try:
        xs = [d.coords[0] for d in devices[0]]
        ys = [d.coords[1] for d in devices[0]]
        wide = len(set(xs))
        tall = devices.shape[1] // wide
        grid_x = np.array(xs).reshape(tall, wide)
        grid_y = np.array(ys).reshape(tall, wide)
        ok = (
            wide * tall == devices.shape[1]
            and wide > 1
            and tall > 1
            and (grid_x == grid_x[:1]).all()
            and (grid_y == grid_y[:, :1]).all()
        )
    except (AttributeError, TypeError, IndexError, ValueError):
        ok = False
    if ok:
        view = devices.reshape(groups, encoders, tall, wide)
        return Mesh(view, ("sg", "sr", "my", "mx")), ("my", "mx"), ("mx", "my")
    view = devices.reshape(groups, encoders, devices.shape[1])
    return Mesh(view, ("sg", "sr", "mp")), "mp", ("mp",)


def solution(mesh):
    inner, mp, stages = split_mesh(mesh)
    seg = ("sg", "sr")
    placed = (
        P(seg, None, None, mp),
        P(seg, None, mp),
        P(seg, None, None, mp),
        P(seg, None, None, None),
    )
    return jax.shard_map(
        functools.partial(per_device, mp, stages),
        mesh=inner,
        in_specs=placed,
        out_specs=(P(seg, None, mp), P(seg, None, mp), P(None, None, mp)),
        check_vma=False,
    )
```
